32 devices in a mesh: face: 4 (over y, x), tile: 8 (over z, core).
Axes of the slice: x: 2, y: 2, z: 4, core: 2. Of those that a mesh axis runs over, the one named last changes fastest.
Arguments:
- inputs: bfloat16 [4, 8, 8, 16, 192], P('face', 'tile'), may hold values from -6 to 6
- upstream: bfloat16 [4, 8, 8, 16, 384], P('face', 'tile'), may hold values from -6 to 6
- weight_in: bfloat16 [3, 3, 192, 384], replicated, may hold values from -0.15625 to 0.15625
- weight_out: bfloat16 [3, 3, 384, 384], replicated, may hold values from -0.109375 to 0.109375
- seam_link: int32 [4, 4], replicated, may hold values from 0 to 15, as said below
- seam_turn: int32 [4, 4], replicated, may hold values from 0 to 1, as said below
Outputs:
- grad_hidden: bfloat16 [4, 8, 8, 16, 384], P('face', 'tile')
- update_in: bfloat16 [3, 3, 192, 384], replicated
- update_out: bfloat16 [3, 3, 384, 384], replicated
The draws below stay inside these ranges and needn't reach their ends.
Inputs may be any that keep to these rules, and one draw needn't show every extreme that they name: The seams pair all 16 sides: if seam_link[f, s] = 4 g + q then (g, q) differs from (f, s) and seam_link[g, q] = 4 f + s. seam_turn is equal on the two sides of every seam.
All inputs are finite; a program needn't handle non-finite values.
Results may differ from the reference program's by a relative error of at most 0.0062.
Values may be sent and summed in bfloat16 or wider, within the bound.
No kernel may reach another device: no remote copies, remote signals or barrier semaphores. Data moves between devices by JAX's collectives and lax.ppermute only.
A program may use at most 128 MiB of HBM per device.

```python
from functools import partial
import jax
import jax.numpy as jnp
from jax import lax

C0 = 192
C1 = 384
TW = 16
TH = 8
ACROSS = 2
SIDE = 32
FACES = 4
TILES = 8
ENTRIES = 1990656


def seam_pairs(key):
    count = 4 * FACES
    scores = jax.random.permutation(jax.random.fold_in(key, 7), count).astype(jnp.int32)
    near_face = jax.random.randint(jax.random.fold_in(key, 11), (), 0, FACES // 2).astype(jnp.int32)
    sides = jax.random.randint(jax.random.fold_in(key, 13), (2,), 0, 4).astype(jnp.int32)
    first_id = 4 * near_face + sides[0]
    second_id = 4 * (near_face + FACES // 2) + sides[1]
    scores = scores.at[first_id].set(-2).at[second_id].set(-1)
    order = jnp.argsort(scores, stable=True).astype(jnp.int32)
    first_side = order[0::2]
    second_side = order[1::2]
    links = jnp.zeros((count,), jnp.int32).at[first_side].set(second_side).at[second_side].set(first_side)
    pair_turn = (jnp.arange(2 * FACES, dtype=jnp.int32) % 2).astype(jnp.int32)
    turns = jnp.zeros((count,), jnp.int32).at[first_side].set(pair_turn).at[second_side].set(pair_turn)
    return (links.reshape(FACES, 4), turns.reshape(FACES, 4))


def draw_seam_link(key, part):
    return seam_pairs(key)[0]


def draw_seam_turn(key, part):
    return seam_pairs(key)[1]


def block_scale(own_key, shape, shards, low, largest):
    loudness, own = 1.0, jax.random.fold_in(own_key, 6)
    for axis_at, blocks in shards:
        steps = jnp.exp(jax.random.uniform(jax.random.fold_in(own, axis_at), (blocks,), jnp.float32, low / len(shards), largest / len(shards)))
        loudness = loudness * jnp.repeat(steps, shape[axis_at] // blocks).reshape([-1 if axis == axis_at else 1 for axis in range(len(shape))])
    return loudness


def bell_draw(rng, shape, deviation, limit, shards=(), kind=jnp.bfloat16):
    factor_of = block_scale(rng, shape, shards, -0.22, 0.18) if shards else 1.0
    result = jax.random.normal(rng, shape, jnp.float32) * deviation * factor_of
    return jnp.minimum(jnp.maximum(result, -limit), limit).astype(kind)


def setup_inputs(seed: int = 0) -> dict:
    arg_keys = jax.random.split(jax.random.key(seed), 7)
    inputs = bell_draw(arg_keys[0], (FACES, TILES, TH, TW, C0), 1.0, 6.0, ((0, 4), (1, 8)))
    upstream = bell_draw(arg_keys[1], (FACES, TILES, TH, TW, C1), 1.0, 6.0, ((0, 4), (1, 8)))
    weight_in = bell_draw(arg_keys[2], (3, 3, C0, C1), (9 * C0) ** -0.5, 0.15625)
    weight_out = bell_draw(arg_keys[3], (3, 3, C1, C1), (9 * C1) ** -0.5, 0.109375)
    seam_link = draw_seam_link(jax.random.fold_in(arg_keys[6], 71), 0)
    seam_turn = draw_seam_turn(jax.random.fold_in(arg_keys[6], 71), 0)
    return dict(inputs=inputs, upstream=upstream, weight_in=weight_in, weight_out=weight_out, seam_link=seam_link, seam_turn=seam_turn)


root_half = 0.7071067811865476
inv_root_tau = 0.3989422804014327
epsilon = 1e-06

def gelu_value(pre):
    return pre * 0.5 * (1.0 + lax.erf(pre * root_half))

def gelu_slope(pre):
    return 0.5 * (1.0 + lax.erf(pre * root_half)) + pre * jnp.exp(-0.5 * pre * pre) * inv_root_tau

def to_faces(tiles):
    depth = tiles.shape[-1]
    shaped = tiles.reshape(FACES, 4, ACROSS, TH, TW, depth)
    return shaped.transpose(0, 1, 3, 2, 4, 5).reshape(FACES, SIDE, SIDE, depth)

def to_tiles(faces_cells):
    depth = faces_cells.shape[-1]
    shaped = faces_cells.reshape(FACES, 4, TH, ACROSS, TW, depth)
    return shaped.transpose(0, 1, 3, 2, 4, 5).reshape(FACES, TILES, TH, TW, depth)

def pad_faces(field, seam_link, seam_turn):
    depth = field.shape[-1]
    edges = jnp.stack([field[:, 0], field[:, -1], field[:, :, 0], field[:, :, -1]], axis=1)
    flattened = edges.reshape(-1, SIDE, depth)
    picked = jnp.take(flattened, seam_link.reshape(-1), axis=0).reshape(edges.shape)
    halo = jnp.where((seam_turn == 1)[:, :, None, None], picked[:, :, ::-1], picked)
    middle = jnp.concatenate([halo[:, 2][:, :, None], field, halo[:, 3][:, :, None]], axis=2)
    nothing = jnp.zeros_like(halo[:, 0, :1])
    upper = jnp.concatenate([nothing, halo[:, 0], nothing], axis=1)[:, None]
    lower = jnp.concatenate([nothing, halo[:, 1], nothing], axis=1)[:, None]
    return jnp.concatenate([upper, middle, lower], axis=1)

def convolve(padded, weight):

    def one_face(face_cells):
        total = jnp.zeros((SIDE * SIDE, weight.shape[3]), jnp.float32)
        for down_step in range(3):
            for side_step in range(3):
                window = face_cells[down_step:down_step + SIDE, side_step:side_step + SIDE].reshape(SIDE * SIDE, -1)
                total = total + jnp.dot(window, weight[down_step, side_step], precision=lax.Precision.HIGHEST)
        return total
    return lax.map(one_face, padded)

def weight_grad(padded, grads):

    def one_face(pair):
        face_cells, face_grad = pair
        blocks = []
        for down_step in range(3):
            for side_step in range(3):
                window = face_cells[down_step:down_step + SIDE, side_step:side_step + SIDE].reshape(SIDE * SIDE, -1)
                blocks.append(jnp.dot(window.T, face_grad, precision=lax.Precision.HIGHEST))
        return jnp.stack(blocks).reshape(3, 3, face_cells.shape[-1], face_grad.shape[-1])
    return lax.optimization_barrier(jnp.sum(lax.map(one_face, (padded, grads)), axis=0))

def spread_back(grads, weight):

    def one_face(face_grad):
        frame = jnp.zeros((SIDE + 2, SIDE + 2, weight.shape[2]), jnp.float32)
        for down_step in range(3):
            for side_step in range(3):
                piece = jnp.dot(face_grad, weight[down_step, side_step].T, precision=lax.Precision.HIGHEST)
                piece = piece.reshape(SIDE, SIDE, -1)
                frame = frame + jnp.pad(piece, ((down_step, 2 - down_step), (side_step, 2 - side_step), (0, 0)))
        return frame
    return lax.map(one_face, grads)

def reference(inputs, upstream, weight_in, weight_out, seam_link, seam_turn):
    weight_one = weight_in.astype(jnp.float32)
    weight_two = weight_out.astype(jnp.float32)
    padder = partial(pad_faces, seam_link=seam_link, seam_turn=seam_turn)
    padded_in = padder(to_faces(inputs).astype(jnp.float32))
    pre_one = convolve(padded_in, weight_one)
    act = gelu_value(pre_one).astype(jnp.bfloat16)
    act_faces = act.reshape(FACES, SIDE, SIDE, C1).astype(jnp.float32)
    padded_act, pad_back = jax.vjp(padder, act_faces)
    pre_two = convolve(padded_act, weight_two)
    upstream_faces = to_faces(upstream).reshape(FACES, SIDE * SIDE, C1).astype(jnp.float32)
    grad_two = (upstream_faces * gelu_slope(pre_two)).astype(jnp.bfloat16).astype(jnp.float32)
    grad_w_out = weight_grad(padded_act, grad_two)
    frame = spread_back(grad_two, weight_two)
    grad_act, = pad_back(frame)
    grad_one = (grad_act.reshape(FACES, SIDE * SIDE, C1) * gelu_slope(pre_one)).astype(jnp.bfloat16)
    grad_w_in = weight_grad(padded_in, grad_one.astype(jnp.float32))
    squares = jnp.sum(grad_w_in * grad_w_in) + jnp.sum(grad_w_out * grad_w_out)
    factor = lax.rsqrt(squares / ENTRIES + epsilon)
    grad_hidden = to_tiles(grad_one.reshape(FACES, SIDE, SIDE, C1))
    return (grad_hidden, (grad_w_in * factor).astype(jnp.bfloat16), (grad_w_out * factor).astype(jnp.bfloat16))
```

```python
import numpy as np
import jax
import jax.numpy as jnp
from jax import lax
from jax.sharding import PartitionSpec as P

root_half = 0.7071067811865476
inv_root_tau = 0.3989422804014327
epsilon = 1e-06
both = ("face", "tile")


def gelu_value(pre):
    return pre * 0.5 * (1.0 + lax.erf(pre * root_half))


def gelu_slope(pre):
    return 0.5 * (1.0 + lax.erf(pre * root_half)) + pre * jnp.exp(-0.5 * pre * pre) * inv_root_tau


def rim_of(cells):
    return jnp.concatenate([cells[0], cells[-1], cells[:, 0], cells[:, -1]], axis=0)


def border_of(frame):
    return jnp.concatenate([frame[0], frame[-1], frame[1:-1, 0], frame[1:-1, -1]], axis=0)


def halo_sources(seam_link, seam_turn, faces, tiles, height, breadth):
    across = tiles // 4
    side = across * breadth
    rim_len = 2 * (height + breadth)
    a = np.array([0] * (breadth + 2) + [height + 1] * (breadth + 2) + list(range(1, height + 1)) * 2)
    b = np.array(list(range(breadth + 2)) * 2 + [0] * height + [breadth + 1] * height)
    dev = np.arange(faces * tiles)
    f = dev // tiles
    t = dev % tiles
    i = (t // across)[:, None] * height - 1 + a[None, :]
    j = (t % across)[:, None] * breadth - 1 + b[None, :]
    out_i = (i < 0) | (i >= side)
    out_j = (j < 0) | (j >= side)
    corner = out_i & out_j
    seam = (out_i | out_j) & ~corner
    s = np.where(i < 0, 0, np.where(i >= side, 1, np.where(j < 0, 2, 3)))
    p = np.where(out_i, j, i)
    fb = np.broadcast_to(f[:, None], i.shape)
    link = seam_link[fb, s]
    turn = seam_turn[fb, s]
    g = link // 4
    q = link % 4
    pp = jnp.where(turn == 1, side - 1 - p, p)
    si = jnp.where(q == 0, 0, jnp.where(q == 1, side - 1, pp))
    sj = jnp.where(q == 2, 0, jnp.where(q == 3, side - 1, pp))
    src_face = jnp.where(seam, g, fb)
    src_i = jnp.clip(jnp.where(seam, si, i), 0, side - 1)
    src_j = jnp.clip(jnp.where(seam, sj, j), 0, side - 1)
    li = src_i % height
    lj = src_j % breadth
    rim_idx = jnp.where(
        li == 0,
        lj,
        jnp.where(
            li == height - 1,
            breadth + lj,
            jnp.where(lj == 0, 2 * breadth + li, 2 * breadth + height + li),
        ),
    )
    tile_of = (src_i // height) * across + src_j // breadth
    gid = (src_face * tiles + tile_of) * rim_len + rim_idx
    return jnp.where(corner, -1, gid).astype(jnp.int32)


def padded_tile(cells, own_src):
    height, breadth, depth = cells.shape
    rims = lax.all_gather(rim_of(cells), both, axis=0, tiled=True)
    count = rims.shape[0]
    rims = jnp.concatenate([rims, jnp.zeros((1, depth), rims.dtype)], axis=0)
    halo = jnp.take(rims, jnp.where(own_src < 0, count, own_src), axis=0)
    upper = halo[: breadth + 2]
    lower = halo[breadth + 2 : 2 * breadth + 4]
    left_side = halo[2 * breadth + 4 : 2 * breadth + 4 + height]
    right_side = halo[2 * breadth + 4 + height :]
    middle = jnp.concatenate([left_side[:, None], cells, right_side[:, None]], axis=1)
    return jnp.concatenate([upper[None], middle, lower[None]], axis=0)


def unfold(padded, height, breadth):
    depth = padded.shape[2]
    windows = []
    for down_step in range(3):
        for side_step in range(3):
            windows.append(
                padded[down_step : down_step + height, side_step : side_step + breadth].reshape(
                    height * breadth, depth
                )
            )
    return jnp.concatenate(windows, axis=1)


def body(inputs, upstream, weight_in, weight_out, seam_link, seam_turn):
    cells = inputs[0, 0]
    height, breadth, width_in = cells.shape
    width_out = weight_out.shape[3]
    faces = lax.axis_size("face")
    tiles = lax.axis_size("tile")
    rim_len = 2 * (height + breadth)
    device = lax.axis_index("face") * tiles + lax.axis_index("tile")
    sources = halo_sources(seam_link, seam_turn, faces, tiles, height, breadth)
    own_src = lax.dynamic_index_in_dim(sources, device, 0, False)
    unfolded_in = unfold(padded_tile(cells, own_src), height, breadth)
    pre_one = jnp.dot(
        unfolded_in, weight_in.reshape(-1, width_out), preferred_element_type=jnp.float32
    )
    act = gelu_value(pre_one).astype(jnp.bfloat16)
    padded_act = padded_tile(act.reshape(height, breadth, width_out), own_src)
    unfolded_act = unfold(padded_act, height, breadth)
    kernel_out = weight_out.reshape(-1, width_out)
    pre_two = jnp.dot(unfolded_act, kernel_out, preferred_element_type=jnp.float32)
    grad_two = (upstream[0, 0].reshape(-1, width_out) * gelu_slope(pre_two)).astype(jnp.bfloat16)
    grad_w_out = lax.dot_general(
        unfolded_act, grad_two, (((0,), (0,)), ((), ())), preferred_element_type=jnp.float32
    )
    spread = lax.dot_general(
        grad_two, kernel_out, (((1,), (1,)), ((), ())), preferred_element_type=jnp.float32
    )
    frame = jnp.zeros((height + 2, breadth + 2, width_out), jnp.float32)
    for down_step in range(3):
        for side_step in range(3):
            offset = (down_step * 3 + side_step) * width_out
            piece = spread[:, offset : offset + width_out].reshape(height, breadth, width_out)
            frame = frame + jnp.pad(
                piece, ((down_step, 2 - down_step), (side_step, 2 - side_step), (0, 0))
            )
    borders = lax.all_gather(border_of(frame), both, axis=0, tiled=True)
    borders, grad_w_out = lax.optimization_barrier((borders, grad_w_out))
    total_out = lax.psum(grad_w_out, both)
    own_cells = device * rim_len + jnp.arange(rim_len, dtype=jnp.int32)
    picker = (sources.reshape(1, -1) == own_cells[:, None]).astype(jnp.float32)
    own_rim = jnp.dot(picker, borders, precision=lax.Precision.HIGHEST)
    _, rim_back = jax.vjp(rim_of, jnp.zeros((height, breadth, width_out), jnp.float32))
    (rim_add,) = rim_back(own_rim)
    grad_act = frame[1:-1, 1:-1] + rim_add
    grad_one = (grad_act * gelu_slope(pre_one.reshape(height, breadth, width_out))).astype(
        jnp.bfloat16
    )
    grad_w_in = lax.dot_general(
        unfolded_in,
        grad_one.reshape(-1, width_out),
        (((0,), (0,)), ((), ())),
        preferred_element_type=jnp.float32,
    )
    total_out, grad_w_in = lax.optimization_barrier((total_out, grad_w_in))
    total_in = lax.psum(grad_w_in, both)
    entries = total_in.size + total_out.size
    squares = jnp.sum(total_in * total_in) + jnp.sum(total_out * total_out)
    factor = lax.rsqrt(squares / entries + epsilon)
    update_in = (total_in * factor).astype(jnp.bfloat16)
    update_out = (total_out * factor).astype(jnp.bfloat16)
    update_in = update_in.reshape(3, 3, width_in, width_out)
    update_out = update_out.reshape(3, 3, width_out, width_out)
    return (grad_one[None, None], update_in, update_out)


def solution(mesh):
    placed = (
        P("face", "tile", None, None, None),
        P("face", "tile", None, None, None),
        P(),
        P(),
        P(),
        P(),
    )
    return jax.shard_map(
        body,
        mesh=mesh,
        in_specs=placed,
        out_specs=(P("face", "tile", None, None, None), P(), P()),
        check_vma=False,
    )
```

```python
import numpy as np
import jax
import jax.numpy as jnp
from jax import lax
from jax.sharding import PartitionSpec as P

root_half = 0.7071067811865476
inv_root_tau = 0.3989422804014327
epsilon = 1e-06


def gelu_value(pre):
    return pre * 0.5 * (1.0 + lax.erf(pre * root_half))


def gelu_slope(pre):
    return 0.5 * (1.0 + lax.erf(pre * root_half)) + pre * jnp.exp(-0.5 * pre * pre) * inv_root_tau


def rim_of(cells):
    return jnp.concatenate([cells[0], cells[-1], cells[:, 0], cells[:, -1]], axis=0)


def border_of(frame):
    return jnp.concatenate([frame[0], frame[-1], frame[1:-1, 0], frame[1:-1, -1]], axis=0)


def rim_index(li, lj, height, breadth):
    return np.where(
        li == 0,
        lj,
        np.where(
            li == height - 1,
            breadth + lj,
            np.where(lj == 0, 2 * breadth + li, 2 * breadth + height + li),
        ),
    )


def face_maps(tiles, height, breadth):
    across = tiles // 4
    side = across * breadth
    rim_len = 2 * (height + breadth)
    a = np.array([0] * (breadth + 2) + [height + 1] * (breadth + 2) + list(range(1, height + 1)) * 2)
    b = np.array(list(range(breadth + 2)) * 2 + [0] * height + [breadth + 1] * height)
    t = np.arange(tiles)
    i = (t // across)[:, None] * height - 1 + a[None, :]
    j = (t % across)[:, None] * breadth - 1 + b[None, :]
    out_i = (i < 0) | (i >= side)
    out_j = (j < 0) | (j >= side)
    inside = ~out_i & ~out_j
    seam = out_i ^ out_j
    ci = np.clip(i, 0, side - 1)
    cj = np.clip(j, 0, side - 1)
    owner = (ci // height) * across + cj // breadth
    intra = np.where(inside, owner * rim_len + rim_index(ci % height, cj % breadth, height, breadth), -1)
    s = np.where(i < 0, 0, np.where(i >= side, 1, np.where(j < 0, 2, 3)))
    p = np.where(out_i, cj, ci)
    seam_cell = np.where(seam, s * side + p, -1)
    pos = np.arange(side)
    ei = np.concatenate([np.zeros(side, int), np.full(side, side - 1), pos, pos])
    ej = np.concatenate([pos, pos, np.zeros(side, int), np.full(side, side - 1)])
    sides = np.repeat(np.arange(4), side)
    li = ei % height
    lj = ej % breadth
    k = np.where(sides == 0, lj, np.where(sides == 1, breadth + lj, np.where(sides == 2, 2 * breadth + li, 2 * breadth + height + li)))
    edge = ((ei // height) * across + ej // breadth) * rim_len + k
    return intra.astype(np.int32), seam_cell.astype(np.int32), edge.astype(np.int32)


def one_hot(rows, cols, dtype):
    return (rows[:, None] == cols[None, :]).astype(dtype)


def halo_lookup(edge_set, link_row, turn_row):
    side_len = edge_set.shape[2]
    depth = edge_set.shape[3]
    flattened = edge_set.reshape(-1, side_len, depth)
    picked = jnp.take(flattened, link_row, axis=0)
    return jnp.where((turn_row == 1)[:, None, None], picked[:, ::-1], picked)


def padded_tile(cells, maps, place, link_row, turn_row):
    height, breadth, depth = cells.shape
    intra, seam_cell, edge = maps
    rim_len = 2 * (height + breadth)
    tiles = intra.shape[0]
    side = edge.shape[0] // 4
    rims = lax.all_gather(rim_of(cells), "tile", axis=0, tiled=True)
    edges = jnp.dot(
        one_hot(jnp.asarray(edge), jnp.arange(tiles * rim_len), cells.dtype),
        rims,
        preferred_element_type=jnp.float32,
    ).astype(cells.dtype)
    edge_set = lax.all_gather(edges.reshape(1, 4, side, depth), "face", axis=0, tiled=True)
    seam_halo = halo_lookup(edge_set, link_row, turn_row).reshape(4 * side, depth)
    own_intra = lax.dynamic_index_in_dim(jnp.asarray(intra), place, 0, False)
    own_seam = lax.dynamic_index_in_dim(jnp.asarray(seam_cell), place, 0, False)
    pool = jnp.concatenate([rims, seam_halo], axis=0)
    source = jnp.where(own_intra >= 0, own_intra, jnp.where(own_seam >= 0, tiles * rim_len + own_seam, -1))
    halo = jnp.dot(
        one_hot(source, jnp.arange(pool.shape[0]), cells.dtype),
        pool,
        preferred_element_type=jnp.float32,
    ).astype(cells.dtype)
    upper = halo[: breadth + 2]
    lower = halo[breadth + 2 : 2 * breadth + 4]
    left_side = halo[2 * breadth + 4 : 2 * breadth + 4 + height]
    right_side = halo[2 * breadth + 4 + height :]
    middle = jnp.concatenate([left_side[:, None], cells, right_side[:, None]], axis=1)
    return jnp.concatenate([upper[None], middle, lower[None]], axis=0)


def return_border(border, maps, place, link_row, turn_row):
    intra, seam_cell, edge = maps
    tiles, frame_len = intra.shape
    depth = border.shape[-1]
    rim_len = frame_len - 4
    side = edge.shape[0] // 4
    exact = lax.Precision.HIGHEST
    borders = lax.all_gather(border, "tile", axis=0, tiled=True)
    seam_sum = jnp.dot(
        one_hot(jnp.arange(4 * side), jnp.asarray(seam_cell.reshape(-1)), jnp.float32),
        borders,
        precision=exact,
    )
    seam_set = lax.all_gather(seam_sum.reshape(1, 4, side, depth), "face", axis=0, tiled=True)
    own_edges = halo_lookup(seam_set, link_row, turn_row).reshape(4 * side, depth)
    own_cells = place * rim_len + jnp.arange(rim_len)
    from_tiles = jnp.dot(
        one_hot(own_cells, jnp.asarray(intra.reshape(-1)), jnp.float32), borders, precision=exact
    )
    from_seams = jnp.dot(
        one_hot(own_cells, jnp.asarray(edge), jnp.float32), own_edges, precision=exact
    )
    return from_tiles + from_seams


def unfold(padded, height, breadth):
    depth = padded.shape[2]
    windows = []
    for down_step in range(3):
        for side_step in range(3):
            windows.append(
                padded[down_step : down_step + height, side_step : side_step + breadth].reshape(
                    height * breadth, depth
                )
            )
    return jnp.concatenate(windows, axis=1)


def body(inputs, upstream, weight_in, weight_out, seam_link, seam_turn):
    cells = inputs[0, 0]
    height, breadth, width_in = cells.shape
    width_out = weight_out.shape[3]
    tiles = lax.axis_size("tile")
    place = lax.axis_index("tile")
    face_pos = lax.axis_index("face")
    link_row = lax.dynamic_index_in_dim(seam_link, face_pos, 0, False)
    turn_row = lax.dynamic_index_in_dim(seam_turn, face_pos, 0, False)
    maps = face_maps(tiles, height, breadth)
    unfolded_in = unfold(padded_tile(cells, maps, place, link_row, turn_row), height, breadth)
    pre_one = jnp.dot(
        unfolded_in, weight_in.reshape(-1, width_out), preferred_element_type=jnp.float32
    )
    act = gelu_value(pre_one).astype(jnp.bfloat16)
    padded_act = padded_tile(
        act.reshape(height, breadth, width_out), maps, place, link_row, turn_row
    )
    unfolded_act = unfold(padded_act, height, breadth)
    kernel_out = weight_out.reshape(-1, width_out)
    pre_two = jnp.dot(unfolded_act, kernel_out, preferred_element_type=jnp.float32)
    grad_two = (upstream[0, 0].reshape(-1, width_out) * gelu_slope(pre_two)).astype(jnp.bfloat16)
    grad_w_out = lax.dot_general(
        unfolded_act, grad_two, (((0,), (0,)), ((), ())), preferred_element_type=jnp.float32
    )
    spread = lax.dot_general(
        grad_two, kernel_out, (((1,), (1,)), ((), ())), preferred_element_type=jnp.float32
    )
    frame = jnp.zeros((height + 2, breadth + 2, width_out), jnp.float32)
    for down_step in range(3):
        for side_step in range(3):
            offset = (down_step * 3 + side_step) * width_out
            piece = spread[:, offset : offset + width_out].reshape(height, breadth, width_out)
            frame = frame + jnp.pad(
                piece, ((down_step, 2 - down_step), (side_step, 2 - side_step), (0, 0))
            )
    own_rim = return_border(border_of(frame), maps, place, link_row, turn_row)
    _, rim_back = jax.vjp(rim_of, jnp.zeros((height, breadth, width_out), jnp.float32))
    (rim_add,) = rim_back(own_rim)
    grad_act = frame[1:-1, 1:-1] + rim_add
    grad_one = (grad_act * gelu_slope(pre_one.reshape(height, breadth, width_out))).astype(
        jnp.bfloat16
    )
    grad_w_in = lax.dot_general(
        unfolded_in,
        grad_one.reshape(-1, width_out),
        (((0,), (0,)), ((), ())),
        preferred_element_type=jnp.float32,
    )
    size_in = grad_w_in.shape[0]
    total = lax.psum(jnp.concatenate([grad_w_in, grad_w_out], axis=0), ("face", "tile"))
    factor = lax.rsqrt(jnp.sum(total * total) / total.size + epsilon)
    update = (total * factor).astype(jnp.bfloat16)
    update_in = update[:size_in].reshape(3, 3, width_in, width_out)
    update_out = update[size_in:].reshape(3, 3, width_out, width_out)
    return (grad_one[None, None], update_in, update_out)


def solution(mesh):
    placed = (
        P("face", "tile", None, None, None),
        P("face", "tile", None, None, None),
        P(),
        P(),
        P(),
        P(),
    )
    return jax.shard_map(
        body,
        mesh=mesh,
        in_specs=placed,
        out_specs=(P("face", "tile", None, None, None), P(), P()),
        check_vma=False,
    )
```

```python
import numpy as np
import jax
import jax.numpy as jnp
from jax import lax
from jax.sharding import PartitionSpec as P

root_half = 0.7071067811865476
inv_root_tau = 0.3989422804014327
epsilon = 1e-06


def gelu_value(pre):
    return pre * 0.5 * (1.0 + lax.erf(pre * root_half))


def gelu_slope(pre):
    return 0.5 * (1.0 + lax.erf(pre * root_half)) + pre * jnp.exp(-0.5 * pre * pre) * inv_root_tau


def rim_of(cells):
    return jnp.concatenate([cells[0], cells[-1], cells[:, 0], cells[:, -1]], axis=0)


def border_of(frame):
    return jnp.concatenate([frame[0], frame[-1], frame[1:-1, 0], frame[1:-1, -1]], axis=0)


def rim_index(li, lj, height, breadth):
    return np.where(
        li == 0,
        lj,
        np.where(
            li == height - 1,
            breadth + lj,
            np.where(lj == 0, 2 * breadth + li, 2 * breadth + height + li),
        ),
    )


def face_maps(tiles, height, breadth):
    across = tiles // 4
    side = across * breadth
    rim_len = 2 * (height + breadth)
    a = np.array([0] * (breadth + 2) + [height + 1] * (breadth + 2) + list(range(1, height + 1)) * 2)
    b = np.array(list(range(breadth + 2)) * 2 + [0] * height + [breadth + 1] * height)
    t = np.arange(tiles)
    i = (t // across)[:, None] * height - 1 + a[None, :]
    j = (t % across)[:, None] * breadth - 1 + b[None, :]
    out_i = (i < 0) | (i >= side)
    out_j = (j < 0) | (j >= side)
    inside = ~out_i & ~out_j
    seam = out_i ^ out_j
    ci = np.clip(i, 0, side - 1)
    cj = np.clip(j, 0, side - 1)
    owner = (ci // height) * across + cj // breadth
    intra = np.where(inside, owner * rim_len + rim_index(ci % height, cj % breadth, height, breadth), -1)
    s = np.where(i < 0, 0, np.where(i >= side, 1, np.where(j < 0, 2, 3)))
    p = np.where(out_i, cj, ci)
    seam_cell = np.where(seam, s * side + p, -1)
    pos = np.arange(side)
    ei = np.concatenate([np.zeros(side, int), np.full(side, side - 1), pos, pos])
    ej = np.concatenate([pos, pos, np.zeros(side, int), np.full(side, side - 1)])
    sides = np.repeat(np.arange(4), side)
    li = ei % height
    lj = ej % breadth
    k = np.where(sides == 0, lj, np.where(sides == 1, breadth + lj, np.where(sides == 2, 2 * breadth + li, 2 * breadth + height + li)))
    edge = ((ei // height) * across + ej // breadth) * rim_len + k
    return intra.astype(np.int32), seam_cell.astype(np.int32), edge.astype(np.int32)


def one_hot(rows, cols, dtype):
    return (rows[:, None] == cols[None, :]).astype(dtype)


def halo_lookup(edge_set, link_row, turn_row):
    side_len = edge_set.shape[2]
    depth = edge_set.shape[3]
    flattened = edge_set.reshape(-1, side_len, depth)
    picked = jnp.take(flattened, link_row, axis=0)
    return jnp.where((turn_row == 1)[:, None, None], picked[:, ::-1], picked)


def padded_tile(cells, maps, place, link_row, turn_row):
    height, breadth, depth = cells.shape
    intra, seam_cell, edge = maps
    rim_len = 2 * (height + breadth)
    tiles = intra.shape[0]
    side = edge.shape[0] // 4
    rims = lax.all_gather(rim_of(cells), "tile", axis=0, tiled=True)
    edges = jnp.dot(
        one_hot(jnp.asarray(edge), jnp.arange(tiles * rim_len), cells.dtype),
        rims,
        preferred_element_type=jnp.float32,
    ).astype(cells.dtype)
    edge_set = lax.all_gather(edges.reshape(1, 4, side, depth), "face", axis=0, tiled=True)
    seam_halo = halo_lookup(edge_set, link_row, turn_row).reshape(4 * side, depth)
    own_intra = lax.dynamic_index_in_dim(jnp.asarray(intra), place, 0, False)
    own_seam = lax.dynamic_index_in_dim(jnp.asarray(seam_cell), place, 0, False)
    pool = jnp.concatenate([rims, seam_halo], axis=0)
    source = jnp.where(own_intra >= 0, own_intra, jnp.where(own_seam >= 0, tiles * rim_len + own_seam, -1))
    halo = jnp.dot(
        one_hot(source, jnp.arange(pool.shape[0]), cells.dtype),
        pool,
        preferred_element_type=jnp.float32,
    ).astype(cells.dtype)
    upper = halo[: breadth + 2]
    lower = halo[breadth + 2 : 2 * breadth + 4]
    left_side = halo[2 * breadth + 4 : 2 * breadth + 4 + height]
    right_side = halo[2 * breadth + 4 + height :]
    middle = jnp.concatenate([left_side[:, None], cells, right_side[:, None]], axis=1)
    return jnp.concatenate([upper[None], middle, lower[None]], axis=0)


def return_border(border, maps, place, link_row, turn_row):
    intra, seam_cell, edge = maps
    tiles, frame_len = intra.shape
    depth = border.shape[-1]
    rim_len = frame_len - 4
    side = edge.shape[0] // 4
    exact = lax.Precision.HIGHEST
    borders = lax.all_gather(border, "tile", axis=0, tiled=True)
    seam_sum = jnp.dot(
        one_hot(jnp.arange(4 * side), jnp.asarray(seam_cell.reshape(-1)), jnp.float32),
        borders,
        precision=exact,
    )
    seam_set = lax.all_gather(seam_sum.reshape(1, 4, side, depth), "face", axis=0, tiled=True)
    own_edges = halo_lookup(seam_set, link_row, turn_row).reshape(4 * side, depth)
    own_cells = place * rim_len + jnp.arange(rim_len)
    from_tiles = jnp.dot(
        one_hot(own_cells, jnp.asarray(intra.reshape(-1)), jnp.float32), borders, precision=exact
    )
    from_seams = jnp.dot(
        one_hot(own_cells, jnp.asarray(edge), jnp.float32), own_edges, precision=exact
    )
    return from_tiles + from_seams


def unfold(padded, height, breadth):
    depth = padded.shape[2]
    windows = []
    for down_step in range(3):
        for side_step in range(3):
            windows.append(
                padded[down_step : down_step + height, side_step : side_step + breadth].reshape(
                    height * breadth, depth
                )
            )
    return jnp.concatenate(windows, axis=1)


def body(inputs, upstream, weight_in, weight_out, seam_link, seam_turn):
    cells = inputs[0, 0]
    height, breadth, width_in = cells.shape
    width_out = weight_out.shape[3]
    tiles = lax.axis_size("tile")
    place = lax.axis_index("tile")
    face_pos = lax.axis_index("face")
    link_row = lax.dynamic_index_in_dim(seam_link, face_pos, 0, False)
    turn_row = lax.dynamic_index_in_dim(seam_turn, face_pos, 0, False)
    maps = face_maps(tiles, height, breadth)
    unfolded_in = unfold(padded_tile(cells, maps, place, link_row, turn_row), height, breadth)
    pre_one = jnp.dot(
        unfolded_in, weight_in.reshape(-1, width_out), preferred_element_type=jnp.float32
    )
    act = gelu_value(pre_one).astype(jnp.bfloat16)
    padded_act = padded_tile(
        act.reshape(height, breadth, width_out), maps, place, link_row, turn_row
    )
    unfolded_act = unfold(padded_act, height, breadth)
    kernel_out = weight_out.reshape(-1, width_out)
    pre_two = jnp.dot(unfolded_act, kernel_out, preferred_element_type=jnp.float32)
    grad_two = (upstream[0, 0].reshape(-1, width_out) * gelu_slope(pre_two)).astype(jnp.bfloat16)
    grad_w_out = lax.dot_general(
        unfolded_act, grad_two, (((0,), (0,)), ((), ())), preferred_element_type=jnp.float32
    )
    spread = lax.dot_general(
        grad_two, kernel_out, (((1,), (1,)), ((), ())), preferred_element_type=jnp.float32
    )
    frame = jnp.zeros((height + 2, breadth + 2, width_out), jnp.float32)
    for down_step in range(3):
        for side_step in range(3):
            offset = (down_step * 3 + side_step) * width_out
            piece = spread[:, offset : offset + width_out].reshape(height, breadth, width_out)
            frame = frame + jnp.pad(
                piece, ((down_step, 2 - down_step), (side_step, 2 - side_step), (0, 0))
            )
    own_rim = return_border(border_of(frame), maps, place, link_row, turn_row)
    _, rim_back = jax.vjp(rim_of, jnp.zeros((height, breadth, width_out), jnp.float32))
    (rim_add,) = rim_back(own_rim)
    grad_act = frame[1:-1, 1:-1] + rim_add
    grad_one = (grad_act * gelu_slope(pre_one.reshape(height, breadth, width_out))).astype(
        jnp.bfloat16
    )
    grad_w_in = lax.dot_general(
        unfolded_in,
        grad_one.reshape(-1, width_out),
        (((0,), (0,)), ((), ())),
        preferred_element_type=jnp.float32,
    )
    size_in = grad_w_in.shape[0]
    partial = jnp.concatenate([grad_w_in, grad_w_out], axis=0).astype(jnp.bfloat16)
    total = lax.psum(partial, ("face", "tile")).astype(jnp.float32)
    factor = lax.rsqrt(jnp.sum(total * total) / total.size + epsilon)
    update = (total * factor).astype(jnp.bfloat16)
    update_in = update[:size_in].reshape(3, 3, width_in, width_out)
    update_out = update[size_in:].reshape(3, 3, width_out, width_out)
    return (grad_one[None, None], update_in, update_out)


def solution(mesh):
    placed = (
        P("face", "tile", None, None, None),
        P("face", "tile", None, None, None),
        P(),
        P(),
        P(),
        P(),
    )
    return jax.shard_map(
        body,
        mesh=mesh,
        in_specs=placed,
        out_specs=(P("face", "tile", None, None, None), P(), P()),
        check_vma=False,
    )
```

```python
import numpy as np
import jax
import jax.numpy as jnp
from jax import lax
from jax.sharding import PartitionSpec as P

root_half = 0.7071067811865476
inv_root_tau = 0.3989422804014327
epsilon = 1e-06


def gelu_value(pre):
    return pre * 0.5 * (1.0 + lax.erf(pre * root_half))


def gelu_slope(pre):
    return 0.5 * (1.0 + lax.erf(pre * root_half)) + pre * jnp.exp(-0.5 * pre * pre) * inv_root_tau


def rim_of(cells):
    return jnp.concatenate([cells[0], cells[-1], cells[:, 0], cells[:, -1]], axis=0)


def border_of(frame):
    return jnp.concatenate([frame[0], frame[-1], frame[1:-1, 0], frame[1:-1, -1]], axis=0)


def rim_index(li, lj, height, breadth):
    return np.where(
        li == 0,
        lj,
        np.where(
            li == height - 1,
            breadth + lj,
            np.where(lj == 0, 2 * breadth + li, 2 * breadth + height + li),
        ),
    )


def face_maps(tiles, height, breadth):
    across = tiles // 4
    side = across * breadth
    rim_len = 2 * (height + breadth)
    a = np.array([0] * (breadth + 2) + [height + 1] * (breadth + 2) + list(range(1, height + 1)) * 2)
    b = np.array(list(range(breadth + 2)) * 2 + [0] * height + [breadth + 1] * height)
    t = np.arange(tiles)
    i = (t // across)[:, None] * height - 1 + a[None, :]
    j = (t % across)[:, None] * breadth - 1 + b[None, :]
    out_i = (i < 0) | (i >= side)
    out_j = (j < 0) | (j >= side)
    inside = ~out_i & ~out_j
    seam = out_i ^ out_j
    ci = np.clip(i, 0, side - 1)
    cj = np.clip(j, 0, side - 1)
    owner = (ci // height) * across + cj // breadth
    intra = np.where(inside, owner * rim_len + rim_index(ci % height, cj % breadth, height, breadth), -1)
    s = np.where(i < 0, 0, np.where(i >= side, 1, np.where(j < 0, 2, 3)))
    p = np.where(out_i, cj, ci)
    seam_cell = np.where(seam, s * side + p, -1)
    pos = np.arange(side)
    ei = np.concatenate([np.zeros(side, int), np.full(side, side - 1), pos, pos])
    ej = np.concatenate([pos, pos, np.zeros(side, int), np.full(side, side - 1)])
    sides = np.repeat(np.arange(4), side)
    li = ei % height
    lj = ej % breadth
    k = np.where(sides == 0, lj, np.where(sides == 1, breadth + lj, np.where(sides == 2, 2 * breadth + li, 2 * breadth + height + li)))
    edge = ((ei // height) * across + ej // breadth) * rim_len + k
    return intra.astype(np.int32), seam_cell.astype(np.int32), edge.astype(np.int32)


def one_hot(rows, cols, dtype):
    return (rows[:, None] == cols[None, :]).astype(dtype)


def halo_lookup(edge_set, link_row, turn_row):
    side_len = edge_set.shape[2]
    depth = edge_set.shape[3]
    flattened = edge_set.reshape(-1, side_len, depth)
    picked = jnp.take(flattened, link_row, axis=0)
    return jnp.where((turn_row == 1)[:, None, None], picked[:, ::-1], picked)


def padded_tile(cells, maps, place, link_row, turn_row):
    height, breadth, depth = cells.shape
    intra, seam_cell, edge = maps
    rim_len = 2 * (height + breadth)
    tiles = intra.shape[0]
    side = edge.shape[0] // 4
    rims = lax.all_gather(rim_of(cells), "tile", axis=0, tiled=True)
    edges = jnp.dot(
        one_hot(jnp.asarray(edge), jnp.arange(tiles * rim_len), cells.dtype),
        rims,
        preferred_element_type=jnp.float32,
    ).astype(cells.dtype)
    edge_set = lax.all_gather(edges.reshape(1, 4, side, depth), "face", axis=0, tiled=True)
    seam_halo = halo_lookup(edge_set, link_row, turn_row).reshape(4 * side, depth)
    own_intra = lax.dynamic_index_in_dim(jnp.asarray(intra), place, 0, False)
    own_seam = lax.dynamic_index_in_dim(jnp.asarray(seam_cell), place, 0, False)
    pool = jnp.concatenate([rims, seam_halo], axis=0)
    source = jnp.where(own_intra >= 0, own_intra, jnp.where(own_seam >= 0, tiles * rim_len + own_seam, -1))
    halo = jnp.dot(
        one_hot(source, jnp.arange(pool.shape[0]), cells.dtype),
        pool,
        preferred_element_type=jnp.float32,
    ).astype(cells.dtype)
    upper = halo[: breadth + 2]
    lower = halo[breadth + 2 : 2 * breadth + 4]
    left_side = halo[2 * breadth + 4 : 2 * breadth + 4 + height]
    right_side = halo[2 * breadth + 4 + height :]
    middle = jnp.concatenate([left_side[:, None], cells, right_side[:, None]], axis=1)
    return jnp.concatenate([upper[None], middle, lower[None]], axis=0)


def return_border(border, maps, place, link_row, turn_row):
    intra, seam_cell, edge = maps
    tiles, frame_len = intra.shape
    depth = border.shape[-1]
    rim_len = frame_len - 4
    side = edge.shape[0] // 4
    exact = lax.Precision.HIGHEST
    borders = lax.all_gather(border, "tile", axis=0, tiled=True)
    seam_sum = jnp.dot(
        one_hot(jnp.arange(4 * side), jnp.asarray(seam_cell.reshape(-1)), jnp.float32),
        borders,
        precision=exact,
    )
    seam_set = lax.all_gather(seam_sum.reshape(1, 4, side, depth), "face", axis=0, tiled=True)
    own_edges = halo_lookup(seam_set, link_row, turn_row).reshape(4 * side, depth)
    own_cells = place * rim_len + jnp.arange(rim_len)
    from_tiles = jnp.dot(
        one_hot(own_cells, jnp.asarray(intra.reshape(-1)), jnp.float32), borders, precision=exact
    )
    from_seams = jnp.dot(
        one_hot(own_cells, jnp.asarray(edge), jnp.float32), own_edges, precision=exact
    )
    return from_tiles + from_seams


def unfold(padded, height, breadth):
    depth = padded.shape[2]
    windows = []
    for down_step in range(3):
        for side_step in range(3):
            windows.append(
                padded[down_step : down_step + height, side_step : side_step + breadth].reshape(
                    height * breadth, depth
                )
            )
    return jnp.concatenate(windows, axis=1)


def weight_slice(padded, grads, tiles):
    rows, cols, depth = padded.shape
    part = depth // tiles
    pieces = padded.reshape(rows, cols, tiles, part).transpose(2, 0, 1, 3)
    mine = lax.all_to_all(pieces, "tile", 0, 0, tiled=True)
    every_grad = lax.all_gather(grads, "tile", axis=0, tiled=True)
    windows = jax.vmap(lambda one: unfold(one, rows - 2, cols - 2))(mine)
    windows = windows.reshape(-1, windows.shape[-1])
    return lax.dot_general(
        windows, every_grad, (((0,), (0,)), ((), ())), preferred_element_type=jnp.float32
    )


def body(inputs, upstream, weight_in, weight_out, seam_link, seam_turn):
    cells = inputs[0, 0]
    height, breadth, width_in = cells.shape
    width_out = weight_out.shape[3]
    tiles = lax.axis_size("tile")
    place = lax.axis_index("tile")
    face_pos = lax.axis_index("face")
    link_row = lax.dynamic_index_in_dim(seam_link, face_pos, 0, False)
    turn_row = lax.dynamic_index_in_dim(seam_turn, face_pos, 0, False)
    maps = face_maps(tiles, height, breadth)
    padded_tile_in = padded_tile(cells, maps, place, link_row, turn_row)
    unfolded_in = unfold(padded_tile_in, height, breadth)
    pre_one = jnp.dot(
        unfolded_in, weight_in.reshape(-1, width_out), preferred_element_type=jnp.float32
    )
    act = gelu_value(pre_one).astype(jnp.bfloat16)
    padded_act = padded_tile(
        act.reshape(height, breadth, width_out), maps, place, link_row, turn_row
    )
    unfolded_act = unfold(padded_act, height, breadth)
    kernel_out = weight_out.reshape(-1, width_out)
    pre_two = jnp.dot(unfolded_act, kernel_out, preferred_element_type=jnp.float32)
    grad_two = (upstream[0, 0].reshape(-1, width_out) * gelu_slope(pre_two)).astype(jnp.bfloat16)
    spread = lax.dot_general(
        grad_two, kernel_out, (((1,), (1,)), ((), ())), preferred_element_type=jnp.float32
    )
    frame = jnp.zeros((height + 2, breadth + 2, width_out), jnp.float32)
    for down_step in range(3):
        for side_step in range(3):
            offset = (down_step * 3 + side_step) * width_out
            piece = spread[:, offset : offset + width_out].reshape(height, breadth, width_out)
            frame = frame + jnp.pad(
                piece, ((down_step, 2 - down_step), (side_step, 2 - side_step), (0, 0))
            )
    own_rim = return_border(border_of(frame), maps, place, link_row, turn_row)
    _, rim_back = jax.vjp(rim_of, jnp.zeros((height, breadth, width_out), jnp.float32))
    (rim_add,) = rim_back(own_rim)
    grad_act = frame[1:-1, 1:-1] + rim_add
    grad_one = (grad_act * gelu_slope(pre_one.reshape(height, breadth, width_out))).astype(
        jnp.bfloat16
    )
    tile_in = weight_slice(padded_tile_in, grad_one.reshape(-1, width_out), tiles)
    tile_out = weight_slice(padded_act, grad_two, tiles)
    size_in = tile_in.shape[0]
    face_sum = lax.psum(jnp.concatenate([tile_in, tile_out], axis=0), "face")
    total = lax.all_gather(face_sum, "tile", axis=0, tiled=False)
    total_in = total[:, :size_in].reshape(tiles, 9, width_in // tiles, width_out)
    total_out = total[:, size_in:].reshape(tiles, 9, width_out // tiles, width_out)
    total_in = total_in.transpose(1, 0, 2, 3)
    total_out = total_out.transpose(1, 0, 2, 3)
    squares = jnp.sum(total_in * total_in) + jnp.sum(total_out * total_out)
    factor = lax.rsqrt(squares / (total_in.size + total_out.size) + epsilon)
    update_in = (total_in * factor).astype(jnp.bfloat16).reshape(3, 3, width_in, width_out)
    update_out = (total_out * factor).astype(jnp.bfloat16).reshape(3, 3, width_out, width_out)
    return (grad_one[None, None], update_in, update_out)


def solution(mesh):
    placed = (
        P("face", "tile", None, None, None),
        P("face", "tile", None, None, None),
        P(),
        P(),
        P(),
        P(),
    )
    return jax.shard_map(
        body,
        mesh=mesh,
        in_specs=placed,
        out_specs=(P("face", "tile", None, None, None), P(), P()),
        check_vma=False,
    )
```

```python
import numpy as np
import jax
import jax.numpy as jnp
from jax import lax
from jax.sharding import PartitionSpec as P

root_half = 0.7071067811865476
inv_root_tau = 0.3989422804014327
epsilon = 1e-06


def gelu_value(pre):
    return pre * 0.5 * (1.0 + lax.erf(pre * root_half))


def gelu_slope(pre):
    return 0.5 * (1.0 + lax.erf(pre * root_half)) + pre * jnp.exp(-0.5 * pre * pre) * inv_root_tau


def rim_of(cells):
    return jnp.concatenate([cells[0], cells[-1], cells[:, 0], cells[:, -1]], axis=0)


def border_of(frame):
    return jnp.concatenate([frame[0], frame[-1], frame[1:-1, 0], frame[1:-1, -1]], axis=0)


def rim_index(li, lj, height, breadth):
    return np.where(
        li == 0,
        lj,
        np.where(
            li == height - 1,
            breadth + lj,
            np.where(lj == 0, 2 * breadth + li, 2 * breadth + height + li),
        ),
    )


def face_maps(tiles, height, breadth):
    across = tiles // 4
    side = across * breadth
    rim_len = 2 * (height + breadth)
    a = np.array([0] * (breadth + 2) + [height + 1] * (breadth + 2) + list(range(1, height + 1)) * 2)
    b = np.array(list(range(breadth + 2)) * 2 + [0] * height + [breadth + 1] * height)
    t = np.arange(tiles)
    i = (t // across)[:, None] * height - 1 + a[None, :]
    j = (t % across)[:, None] * breadth - 1 + b[None, :]
    out_i = (i < 0) | (i >= side)
    out_j = (j < 0) | (j >= side)
    inside = ~out_i & ~out_j
    seam = out_i ^ out_j
    ci = np.clip(i, 0, side - 1)
    cj = np.clip(j, 0, side - 1)
    owner = (ci // height) * across + cj // breadth
    intra = np.where(inside, owner * rim_len + rim_index(ci % height, cj % breadth, height, breadth), -1)
    s = np.where(i < 0, 0, np.where(i >= side, 1, np.where(j < 0, 2, 3)))
    p = np.where(out_i, cj, ci)
    seam_cell = np.where(seam, s * side + p, -1)
    pos = np.arange(side)
    ei = np.concatenate([np.zeros(side, int), np.full(side, side - 1), pos, pos])
    ej = np.concatenate([pos, pos, np.zeros(side, int), np.full(side, side - 1)])
    sides = np.repeat(np.arange(4), side)
    li = ei % height
    lj = ej % breadth
    k = np.where(sides == 0, lj, np.where(sides == 1, breadth + lj, np.where(sides == 2, 2 * breadth + li, 2 * breadth + height + li)))
    edge = ((ei // height) * across + ej // breadth) * rim_len + k
    edge_of_rim = np.full((tiles, rim_len), -1)
    edge_of_rim[edge // rim_len, edge % rim_len] = np.arange(4 * side)
    maps = (intra, seam_cell, edge, edge_of_rim)
    return tuple(m.astype(np.int32) for m in maps)


def one_hot(rows, cols, dtype):
    return (rows[:, None] == cols[None, :]).astype(dtype)


def seam_source(cell, link_row, turn_row, side):
    which = cell // side
    pos = cell % side
    link = jnp.zeros_like(cell)
    turn = jnp.zeros_like(cell)
    for k in range(4):
        link = jnp.where(which == k, link_row[k], link)
        turn = jnp.where(which == k, turn_row[k], turn)
    return link * side + jnp.where(turn == 1, side - 1 - pos, pos)


def padded_tile(cells, maps, place, link_row, turn_row):
    height, breadth, depth = cells.shape
    intra, seam_cell, edge, _ = maps
    rim_len = 2 * (height + breadth)
    tiles = intra.shape[0]
    side = edge.shape[0] // 4
    rims = lax.all_gather(rim_of(cells), "tile", axis=0, tiled=True)
    edges = jnp.dot(
        one_hot(jnp.asarray(edge), jnp.arange(tiles * rim_len), cells.dtype),
        rims,
        preferred_element_type=jnp.float32,
    ).astype(cells.dtype)
    edge_set = lax.all_gather(edges, "face", axis=0, tiled=True)
    own_intra = lax.dynamic_index_in_dim(jnp.asarray(intra), place, 0, False)
    own_seam = lax.dynamic_index_in_dim(jnp.asarray(seam_cell), place, 0, False)
    pool = jnp.concatenate([rims, edge_set], axis=0)
    glued = tiles * rim_len + seam_source(jnp.maximum(own_seam, 0), link_row, turn_row, side)
    source = jnp.where(own_intra >= 0, own_intra, jnp.where(own_seam >= 0, glued, -1))
    halo = jnp.dot(
        one_hot(source, jnp.arange(pool.shape[0]), cells.dtype),
        pool,
        preferred_element_type=jnp.float32,
    ).astype(cells.dtype)
    upper = halo[: breadth + 2]
    lower = halo[breadth + 2 : 2 * breadth + 4]
    left_side = halo[2 * breadth + 4 : 2 * breadth + 4 + height]
    right_side = halo[2 * breadth + 4 + height :]
    middle = jnp.concatenate([left_side[:, None], cells, right_side[:, None]], axis=1)
    return jnp.concatenate([upper[None], middle, lower[None]], axis=0)


def return_border(border, maps, place, link_row, turn_row):
    intra, seam_cell, edge, edge_of_rim = maps
    tiles, frame_len = intra.shape
    rim_len = frame_len - 4
    side = edge.shape[0] // 4
    exact = lax.Precision.HIGHEST
    borders = lax.all_gather(border, "tile", axis=0, tiled=True)
    seam_sum = jnp.dot(
        one_hot(jnp.arange(4 * side), jnp.asarray(seam_cell.reshape(-1)), jnp.float32),
        borders,
        precision=exact,
    )
    seam_set = lax.all_gather(seam_sum, "face", axis=0, tiled=True)
    own_cells = place * rim_len + jnp.arange(rim_len)
    from_tiles = jnp.dot(
        one_hot(own_cells, jnp.asarray(intra.reshape(-1)), jnp.float32), borders, precision=exact
    )
    own_edge = lax.dynamic_index_in_dim(jnp.asarray(edge_of_rim), place, 0, False)
    glued = seam_source(jnp.maximum(own_edge, 0), link_row, turn_row, side)
    glued = jnp.where(own_edge >= 0, glued, -1)
    from_seams = jnp.dot(
        one_hot(glued, jnp.arange(seam_set.shape[0]), jnp.float32), seam_set, precision=exact
    )
    return from_tiles + from_seams


def unfold(padded, height, breadth):
    depth = padded.shape[2]
    windows = []
    for down_step in range(3):
        for side_step in range(3):
            windows.append(
                padded[down_step : down_step + height, side_step : side_step + breadth].reshape(
                    height * breadth, depth
                )
            )
    return jnp.concatenate(windows, axis=1)


def body(inputs, upstream, weight_in, weight_out, seam_link, seam_turn):
    cells = inputs[0, 0]
    height, breadth, width_in = cells.shape
    width_out = weight_out.shape[3]
    tiles = lax.axis_size("tile")
    place = lax.axis_index("tile")
    face_pos = lax.axis_index("face")
    link_row = lax.dynamic_index_in_dim(seam_link, face_pos, 0, False)
    turn_row = lax.dynamic_index_in_dim(seam_turn, face_pos, 0, False)
    maps = face_maps(tiles, height, breadth)
    unfolded_in = unfold(padded_tile(cells, maps, place, link_row, turn_row), height, breadth)
    pre_one = jnp.dot(
        unfolded_in, weight_in.reshape(-1, width_out), preferred_element_type=jnp.float32
    )
    act = gelu_value(pre_one).astype(jnp.bfloat16)
    padded_act = padded_tile(
        act.reshape(height, breadth, width_out), maps, place, link_row, turn_row
    )
    unfolded_act = unfold(padded_act, height, breadth)
    kernel_out = weight_out.reshape(-1, width_out)
    pre_two = jnp.dot(unfolded_act, kernel_out, preferred_element_type=jnp.float32)
    grad_two = (upstream[0, 0].reshape(-1, width_out) * gelu_slope(pre_two)).astype(jnp.bfloat16)
    grad_w_out = lax.dot_general(
        unfolded_act, grad_two, (((0,), (0,)), ((), ())), preferred_element_type=jnp.float32
    )
    spread = lax.dot_general(
        grad_two, kernel_out, (((1,), (1,)), ((), ())), preferred_element_type=jnp.float32
    )
    frame = jnp.zeros((height + 2, breadth + 2, width_out), jnp.float32)
    for down_step in range(3):
        for side_step in range(3):
            offset = (down_step * 3 + side_step) * width_out
            piece = spread[:, offset : offset + width_out].reshape(height, breadth, width_out)
            frame = frame + jnp.pad(
                piece, ((down_step, 2 - down_step), (side_step, 2 - side_step), (0, 0))
            )
    own_rim = return_border(border_of(frame), maps, place, link_row, turn_row)
    _, rim_back = jax.vjp(rim_of, jnp.zeros((height, breadth, width_out), jnp.float32))
    (rim_add,) = rim_back(own_rim)
    grad_act = frame[1:-1, 1:-1] + rim_add
    grad_one = (grad_act * gelu_slope(pre_one.reshape(height, breadth, width_out))).astype(
        jnp.bfloat16
    )
    grad_w_in = lax.dot_general(
        unfolded_in,
        grad_one.reshape(-1, width_out),
        (((0,), (0,)), ((), ())),
        preferred_element_type=jnp.float32,
    )
    size_in = grad_w_in.shape[0]
    total = lax.psum(jnp.concatenate([grad_w_in, grad_w_out], axis=0), ("face", "tile"))
    factor = lax.rsqrt(jnp.sum(total * total) / total.size + epsilon)
    update_in = (total[:size_in] * factor).astype(jnp.bfloat16)
    update_out = (total[size_in:] * factor).astype(jnp.bfloat16)
    update_in = update_in.reshape(3, 3, width_in, width_out)
    update_out = update_out.reshape(3, 3, width_out, width_out)
    return (grad_one[None, None], update_in, update_out)


def solution(mesh):
    placed = (
        P("face", "tile", None, None, None),
        P("face", "tile", None, None, None),
        P(),
        P(),
        P(),
        P(),
    )
    return jax.shard_map(
        body,
        mesh=mesh,
        in_specs=placed,
        out_specs=(P("face", "tile", None, None, None), P(), P()),
        check_vma=False,
    )
```

```python
import numpy as np
import jax
import jax.numpy as jnp
from jax import lax
from jax.sharding import PartitionSpec as P

root_half = 0.7071067811865476
inv_root_tau = 0.3989422804014327
epsilon = 1e-06
factor_budget = 48 * 2**20


def gelu_value(pre):
    return pre * 0.5 * (1.0 + lax.erf(pre * root_half))


def gelu_slope(pre):
    return 0.5 * (1.0 + lax.erf(pre * root_half)) + pre * jnp.exp(-0.5 * pre * pre) * inv_root_tau


def rim_of(cells):
    return jnp.concatenate([cells[0], cells[-1], cells[:, 0], cells[:, -1]], axis=0)


def border_of(frame):
    return jnp.concatenate([frame[0], frame[-1], frame[1:-1, 0], frame[1:-1, -1]], axis=0)


def rim_index(li, lj, height, breadth):
    return np.where(
        li == 0,
        lj,
        np.where(
            li == height - 1,
            breadth + lj,
            np.where(lj == 0, 2 * breadth + li, 2 * breadth + height + li),
        ),
    )


def face_maps(tiles, height, breadth):
    across = tiles // 4
    side = across * breadth
    rim_len = 2 * (height + breadth)
    a = np.array([0] * (breadth + 2) + [height + 1] * (breadth + 2) + list(range(1, height + 1)) * 2)
    b = np.array(list(range(breadth + 2)) * 2 + [0] * height + [breadth + 1] * height)
    t = np.arange(tiles)
    i = (t // across)[:, None] * height - 1 + a[None, :]
    j = (t % across)[:, None] * breadth - 1 + b[None, :]
    out_i = (i < 0) | (i >= side)
    out_j = (j < 0) | (j >= side)
    inside = ~out_i & ~out_j
    seam = out_i ^ out_j
    ci = np.clip(i, 0, side - 1)
    cj = np.clip(j, 0, side - 1)
    owner = (ci // height) * across + cj // breadth
    intra = np.where(inside, owner * rim_len + rim_index(ci % height, cj % breadth, height, breadth), -1)
    s = np.where(i < 0, 0, np.where(i >= side, 1, np.where(j < 0, 2, 3)))
    p = np.where(out_i, cj, ci)
    seam_cell = np.where(seam, s * side + p, -1)
    pos = np.arange(side)
    ei = np.concatenate([np.zeros(side, int), np.full(side, side - 1), pos, pos])
    ej = np.concatenate([pos, pos, np.zeros(side, int), np.full(side, side - 1)])
    sides = np.repeat(np.arange(4), side)
    li = ei % height
    lj = ej % breadth
    k = np.where(sides == 0, lj, np.where(sides == 1, breadth + lj, np.where(sides == 2, 2 * breadth + li, 2 * breadth + height + li)))
    edge = ((ei // height) * across + ej // breadth) * rim_len + k
    edge_of_rim = np.full((tiles, rim_len), -1)
    edge_of_rim[edge // rim_len, edge % rim_len] = np.arange(4 * side)
    maps = (intra, seam_cell, edge, edge_of_rim)
    return tuple(m.astype(np.int32) for m in maps)


def one_hot(rows, cols, dtype):
    return (rows[:, None] == cols[None, :]).astype(dtype)


def seam_source(cell, link_row, turn_row, side):
    which = cell // side
    pos = cell % side
    link = jnp.zeros_like(cell)
    turn = jnp.zeros_like(cell)
    for k in range(4):
        link = jnp.where(which == k, link_row[k], link)
        turn = jnp.where(which == k, turn_row[k], turn)
    return link * side + jnp.where(turn == 1, side - 1 - pos, pos)


def padded_tile(cells, maps, place, link_row, turn_row):
    height, breadth, depth = cells.shape
    intra, seam_cell, edge, _ = maps
    rim_len = 2 * (height + breadth)
    tiles = intra.shape[0]
    side = edge.shape[0] // 4
    rims = lax.all_gather(rim_of(cells), "tile", axis=0, tiled=True)
    edges = jnp.dot(
        one_hot(jnp.asarray(edge), jnp.arange(tiles * rim_len), cells.dtype),
        rims,
        preferred_element_type=jnp.float32,
    ).astype(cells.dtype)
    edge_set = lax.all_gather(edges, "face", axis=0, tiled=True)
    own_intra = lax.dynamic_index_in_dim(jnp.asarray(intra), place, 0, False)
    own_seam = lax.dynamic_index_in_dim(jnp.asarray(seam_cell), place, 0, False)
    pool = jnp.concatenate([rims, edge_set], axis=0)
    glued = tiles * rim_len + seam_source(jnp.maximum(own_seam, 0), link_row, turn_row, side)
    source = jnp.where(own_intra >= 0, own_intra, jnp.where(own_seam >= 0, glued, -1))
    halo = jnp.dot(
        one_hot(source, jnp.arange(pool.shape[0]), cells.dtype),
        pool,
        preferred_element_type=jnp.float32,
    ).astype(cells.dtype)
    upper = halo[: breadth + 2]
    lower = halo[breadth + 2 : 2 * breadth + 4]
    left_side = halo[2 * breadth + 4 : 2 * breadth + 4 + height]
    right_side = halo[2 * breadth + 4 + height :]
    middle = jnp.concatenate([left_side[:, None], cells, right_side[:, None]], axis=1)
    return jnp.concatenate([upper[None], middle, lower[None]], axis=0)


def return_border(border, maps, place, link_row, turn_row):
    intra, seam_cell, edge, edge_of_rim = maps
    tiles, frame_len = intra.shape
    rim_len = frame_len - 4
    side = edge.shape[0] // 4
    exact = lax.Precision.HIGHEST
    borders = lax.all_gather(border, "tile", axis=0, tiled=True)
    seam_sum = jnp.dot(
        one_hot(jnp.arange(4 * side), jnp.asarray(seam_cell.reshape(-1)), jnp.float32),
        borders,
        precision=exact,
    )
    seam_set = lax.all_gather(seam_sum, "face", axis=0, tiled=True)
    own_cells = place * rim_len + jnp.arange(rim_len)
    from_tiles = jnp.dot(
        one_hot(own_cells, jnp.asarray(intra.reshape(-1)), jnp.float32), borders, precision=exact
    )
    own_edge = lax.dynamic_index_in_dim(jnp.asarray(edge_of_rim), place, 0, False)
    glued = seam_source(jnp.maximum(own_edge, 0), link_row, turn_row, side)
    glued = jnp.where(own_edge >= 0, glued, -1)
    from_seams = jnp.dot(
        one_hot(glued, jnp.arange(seam_set.shape[0]), jnp.float32), seam_set, precision=exact
    )
    return from_tiles + from_seams


def unfold(padded, height, breadth):
    depth = padded.shape[2]
    windows = []
    for down_step in range(3):
        for side_step in range(3):
            windows.append(
                padded[down_step : down_step + height, side_step : side_step + breadth].reshape(
                    height * breadth, depth
                )
            )
    return jnp.concatenate(windows, axis=1)


def gather_all(block, faces):
    local = lax.all_gather(block, "tile", axis=0, tiled=True)
    parts = [local]
    for shift in range(1, faces):
        pairs = [(i, (i + shift) % faces) for i in range(faces)]
        parts.append(lax.ppermute(local, "face", pairs))
    return jnp.concatenate(parts, axis=0)


def body(inputs, upstream, weight_in, weight_out, seam_link, seam_turn):
    cells = inputs[0, 0]
    height, breadth, width_in = cells.shape
    width_out = weight_out.shape[3]
    tiles = lax.axis_size("tile")
    place = lax.axis_index("tile")
    face_pos = lax.axis_index("face")
    link_row = lax.dynamic_index_in_dim(seam_link, face_pos, 0, False)
    turn_row = lax.dynamic_index_in_dim(seam_turn, face_pos, 0, False)
    maps = face_maps(tiles, height, breadth)
    padded_tile_in = padded_tile(cells, maps, place, link_row, turn_row)
    unfolded_in = unfold(padded_tile_in, height, breadth)
    pre_one = jnp.dot(
        unfolded_in, weight_in.reshape(-1, width_out), preferred_element_type=jnp.float32
    )
    act = gelu_value(pre_one).astype(jnp.bfloat16)
    padded_act = padded_tile(
        act.reshape(height, breadth, width_out), maps, place, link_row, turn_row
    )
    unfolded_act = unfold(padded_act, height, breadth)
    kernel_out = weight_out.reshape(-1, width_out)
    pre_two = jnp.dot(unfolded_act, kernel_out, preferred_element_type=jnp.float32)
    grad_two = (upstream[0, 0].reshape(-1, width_out) * gelu_slope(pre_two)).astype(jnp.bfloat16)
    grad_w_out = lax.dot_general(
        unfolded_act, grad_two, (((0,), (0,)), ((), ())), preferred_element_type=jnp.float32
    )
    spread = lax.dot_general(
        grad_two, kernel_out, (((1,), (1,)), ((), ())), preferred_element_type=jnp.float32
    )
    frame = jnp.zeros((height + 2, breadth + 2, width_out), jnp.float32)
    for down_step in range(3):
        for side_step in range(3):
            offset = (down_step * 3 + side_step) * width_out
            piece = spread[:, offset : offset + width_out].reshape(height, breadth, width_out)
            frame = frame + jnp.pad(
                piece, ((down_step, 2 - down_step), (side_step, 2 - side_step), (0, 0))
            )
    own_rim = return_border(border_of(frame), maps, place, link_row, turn_row)
    _, rim_back = jax.vjp(rim_of, jnp.zeros((height, breadth, width_out), jnp.float32))
    (rim_add,) = rim_back(own_rim)
    grad_act = frame[1:-1, 1:-1] + rim_add
    grad_one = (grad_act * gelu_slope(pre_one.reshape(height, breadth, width_out))).astype(
        jnp.bfloat16
    )
    faces = lax.axis_size("face")
    gathered = faces * tiles * (padded_tile_in.size + grad_one.size) * 2
    if gathered <= factor_budget:
        total_out = lax.psum(grad_w_out, ("face", "tile"))
        every_pad = gather_all(padded_tile_in[None], faces)
        every_grad = gather_all(grad_one.reshape(1, -1, width_out), faces)
        every_grad = every_grad.reshape(-1, width_out)
        blocks = []
        for down_step in range(3):
            for side_step in range(3):
                window = every_pad[:, down_step : down_step + height, side_step : side_step + breadth]
                blocks.append(
                    lax.dot_general(
                        window.reshape(-1, width_in),
                        every_grad,
                        (((0,), (0,)), ((), ())),
                        preferred_element_type=jnp.float32,
                    )
                )
        total_in = jnp.concatenate(blocks, axis=0)
    else:
        grad_w_in = lax.dot_general(
            unfolded_in,
            grad_one.reshape(-1, width_out),
            (((0,), (0,)), ((), ())),
            preferred_element_type=jnp.float32,
        )
        size_in = grad_w_in.shape[0]
        total = lax.psum(jnp.concatenate([grad_w_in, grad_w_out], axis=0), ("face", "tile"))
        total_in = total[:size_in]
        total_out = total[size_in:]
    squares = jnp.sum(total_in * total_in) + jnp.sum(total_out * total_out)
    factor = lax.rsqrt(squares / (total_in.size + total_out.size) + epsilon)
    update_in = (total_in * factor).astype(jnp.bfloat16)
    update_out = (total_out * factor).astype(jnp.bfloat16)
    update_in = update_in.reshape(3, 3, width_in, width_out)
    update_out = update_out.reshape(3, 3, width_out, width_out)
    return (grad_one[None, None], update_in, update_out)


def solution(mesh):
    placed = (
        P("face", "tile", None, None, None),
        P("face", "tile", None, None, None),
        P(),
        P(),
        P(),
        P(),
    )
    return jax.shard_map(
        body,
        mesh=mesh,
        in_specs=placed,
        out_specs=(P("face", "tile", None, None, None), P(), P()),
        check_vma=False,
    )
```

```python
import numpy as np
import jax
import jax.numpy as jnp
from jax import lax
from jax.sharding import PartitionSpec as P

root_half = 0.7071067811865476
inv_root_tau = 0.3989422804014327
epsilon = 1e-06
factor_budget = 48 * 2**20


def gelu_value(pre):
    return pre * 0.5 * (1.0 + lax.erf(pre * root_half))


def gelu_slope(pre):
    return 0.5 * (1.0 + lax.erf(pre * root_half)) + pre * jnp.exp(-0.5 * pre * pre) * inv_root_tau


def rim_of(cells):
    return jnp.concatenate([cells[0], cells[-1], cells[:, 0], cells[:, -1]], axis=0)


def border_of(frame):
    return jnp.concatenate([frame[0], frame[-1], frame[1:-1, 0], frame[1:-1, -1]], axis=0)


def rim_index(li, lj, height, breadth):
    return np.where(
        li == 0,
        lj,
        np.where(
            li == height - 1,
            breadth + lj,
            np.where(lj == 0, 2 * breadth + li, 2 * breadth + height + li),
        ),
    )


def face_maps(tiles, height, breadth):
    across = tiles // 4
    side = across * breadth
    rim_len = 2 * (height + breadth)
    a = np.array([0] * (breadth + 2) + [height + 1] * (breadth + 2) + list(range(1, height + 1)) * 2)
    b = np.array(list(range(breadth + 2)) * 2 + [0] * height + [breadth + 1] * height)
    t = np.arange(tiles)
    i = (t // across)[:, None] * height - 1 + a[None, :]
    j = (t % across)[:, None] * breadth - 1 + b[None, :]
    out_i = (i < 0) | (i >= side)
    out_j = (j < 0) | (j >= side)
    inside = ~out_i & ~out_j
    seam = out_i ^ out_j
    ci = np.clip(i, 0, side - 1)
    cj = np.clip(j, 0, side - 1)
    owner = (ci // height) * across + cj // breadth
    intra = np.where(inside, owner * rim_len + rim_index(ci % height, cj % breadth, height, breadth), -1)
    s = np.where(i < 0, 0, np.where(i >= side, 1, np.where(j < 0, 2, 3)))
    p = np.where(out_i, cj, ci)
    seam_cell = np.where(seam, s * side + p, -1)
    pos = np.arange(side)
    ei = np.concatenate([np.zeros(side, int), np.full(side, side - 1), pos, pos])
    ej = np.concatenate([pos, pos, np.zeros(side, int), np.full(side, side - 1)])
    sides = np.repeat(np.arange(4), side)
    li = ei % height
    lj = ej % breadth
    k = np.where(sides == 0, lj, np.where(sides == 1, breadth + lj, np.where(sides == 2, 2 * breadth + li, 2 * breadth + height + li)))
    edge = ((ei // height) * across + ej // breadth) * rim_len + k
    edge_of_rim = np.full((tiles, rim_len), -1)
    edge_of_rim[edge // rim_len, edge % rim_len] = np.arange(4 * side)
    maps = (intra, seam_cell, edge, edge_of_rim)
    return tuple(m.astype(np.int32) for m in maps)


def one_hot(rows, cols, dtype):
    return (rows[:, None] == cols[None, :]).astype(dtype)


def seam_source(cell, link_row, turn_row, side):
    which = cell // side
    pos = cell % side
    link = jnp.zeros_like(cell)
    turn = jnp.zeros_like(cell)
    for k in range(4):
        link = jnp.where(which == k, link_row[k], link)
        turn = jnp.where(which == k, turn_row[k], turn)
    return link * side + jnp.where(turn == 1, side - 1 - pos, pos)


def padded_tile(cells, maps, place, link_row, turn_row):
    height, breadth, depth = cells.shape
    intra, seam_cell, edge, _ = maps
    rim_len = 2 * (height + breadth)
    tiles = intra.shape[0]
    side = edge.shape[0] // 4
    rims = lax.all_gather(rim_of(cells), "tile", axis=0, tiled=True)
    edges = jnp.dot(
        one_hot(jnp.asarray(edge), jnp.arange(tiles * rim_len), cells.dtype),
        rims,
        preferred_element_type=jnp.float32,
    ).astype(cells.dtype)
    edge_set = lax.all_gather(edges, "face", axis=0, tiled=True)
    own_intra = lax.dynamic_index_in_dim(jnp.asarray(intra), place, 0, False)
    own_seam = lax.dynamic_index_in_dim(jnp.asarray(seam_cell), place, 0, False)
    pool = jnp.concatenate([rims, edge_set], axis=0)
    glued = tiles * rim_len + seam_source(jnp.maximum(own_seam, 0), link_row, turn_row, side)
    source = jnp.where(own_intra >= 0, own_intra, jnp.where(own_seam >= 0, glued, -1))
    halo = jnp.dot(
        one_hot(source, jnp.arange(pool.shape[0]), cells.dtype),
        pool,
        preferred_element_type=jnp.float32,
    ).astype(cells.dtype)
    upper = halo[: breadth + 2]
    lower = halo[breadth + 2 : 2 * breadth + 4]
    left_side = halo[2 * breadth + 4 : 2 * breadth + 4 + height]
    right_side = halo[2 * breadth + 4 + height :]
    middle = jnp.concatenate([left_side[:, None], cells, right_side[:, None]], axis=1)
    return jnp.concatenate([upper[None], middle, lower[None]], axis=0)


def return_border(border, maps, place, link_row, turn_row):
    intra, seam_cell, edge, edge_of_rim = maps
    tiles, frame_len = intra.shape
    rim_len = frame_len - 4
    side = edge.shape[0] // 4
    exact = lax.Precision.HIGHEST
    borders = lax.all_gather(border, "tile", axis=0, tiled=True)
    seam_sum = jnp.dot(
        one_hot(jnp.arange(4 * side), jnp.asarray(seam_cell.reshape(-1)), jnp.float32),
        borders,
        precision=exact,
    )
    seam_set = lax.all_gather(seam_sum, "face", axis=0, tiled=True)
    own_cells = place * rim_len + jnp.arange(rim_len)
    from_tiles = jnp.dot(
        one_hot(own_cells, jnp.asarray(intra.reshape(-1)), jnp.float32), borders, precision=exact
    )
    own_edge = lax.dynamic_index_in_dim(jnp.asarray(edge_of_rim), place, 0, False)
    glued = seam_source(jnp.maximum(own_edge, 0), link_row, turn_row, side)
    glued = jnp.where(own_edge >= 0, glued, -1)
    from_seams = jnp.dot(
        one_hot(glued, jnp.arange(seam_set.shape[0]), jnp.float32), seam_set, precision=exact
    )
    return from_tiles + from_seams


def unfold(padded, height, breadth):
    depth = padded.shape[2]
    windows = []
    for down_step in range(3):
        for side_step in range(3):
            windows.append(
                padded[down_step : down_step + height, side_step : side_step + breadth].reshape(
                    height * breadth, depth
                )
            )
    return jnp.concatenate(windows, axis=1)


def grad_one_size(frame):
    return (frame.shape[0] - 2) * (frame.shape[1] - 2) * frame.shape[2]


def gather_all(block, faces):
    local = lax.all_gather(block, "tile", axis=0, tiled=True)
    parts = [local]
    for shift in range(1, faces):
        pairs = [(i, (i + shift) % faces) for i in range(faces)]
        parts.append(lax.ppermute(local, "face", pairs))
    return jnp.concatenate(parts, axis=0)


def body(inputs, upstream, weight_in, weight_out, seam_link, seam_turn):
    cells = inputs[0, 0]
    height, breadth, width_in = cells.shape
    width_out = weight_out.shape[3]
    tiles = lax.axis_size("tile")
    place = lax.axis_index("tile")
    face_pos = lax.axis_index("face")
    link_row = lax.dynamic_index_in_dim(seam_link, face_pos, 0, False)
    turn_row = lax.dynamic_index_in_dim(seam_turn, face_pos, 0, False)
    maps = face_maps(tiles, height, breadth)
    padded_tile_in = padded_tile(cells, maps, place, link_row, turn_row)
    unfolded_in = unfold(padded_tile_in, height, breadth)
    pre_one = jnp.dot(
        unfolded_in, weight_in.reshape(-1, width_out), preferred_element_type=jnp.float32
    )
    act = gelu_value(pre_one).astype(jnp.bfloat16)
    padded_act = padded_tile(
        act.reshape(height, breadth, width_out), maps, place, link_row, turn_row
    )
    unfolded_act = unfold(padded_act, height, breadth)
    kernel_out = weight_out.reshape(-1, width_out)
    pre_two = jnp.dot(unfolded_act, kernel_out, preferred_element_type=jnp.float32)
    grad_two = (upstream[0, 0].reshape(-1, width_out) * gelu_slope(pre_two)).astype(jnp.bfloat16)
    grad_w_out = lax.dot_general(
        unfolded_act, grad_two, (((0,), (0,)), ((), ())), preferred_element_type=jnp.float32
    )
    spread = lax.dot_general(
        grad_two, kernel_out, (((1,), (1,)), ((), ())), preferred_element_type=jnp.float32
    )
    frame = jnp.zeros((height + 2, breadth + 2, width_out), jnp.float32)
    for down_step in range(3):
        for side_step in range(3):
            offset = (down_step * 3 + side_step) * width_out
            piece = spread[:, offset : offset + width_out].reshape(height, breadth, width_out)
            frame = frame + jnp.pad(
                piece, ((down_step, 2 - down_step), (side_step, 2 - side_step), (0, 0))
            )
    def grad_hidden_of(frame):
        own_rim = return_border(border_of(frame), maps, place, link_row, turn_row)
        _, rim_back = jax.vjp(rim_of, jnp.zeros((height, breadth, width_out), jnp.float32))
        (rim_add,) = rim_back(own_rim)
        grad_act = frame[1:-1, 1:-1] + rim_add
        slope = gelu_slope(pre_one.reshape(height, breadth, width_out))
        return (grad_act * slope).astype(jnp.bfloat16)

    faces = lax.axis_size("face")
    gathered = faces * tiles * (padded_tile_in.size + grad_one_size(frame)) * 2
    if gathered <= factor_budget:
        total_out = lax.psum(grad_w_out, ("face", "tile"))

        def rest(frame):
            grad_one = grad_hidden_of(frame)
            every_pad = gather_all(padded_tile_in[None], faces)
            every_grad = gather_all(grad_one.reshape(1, -1, width_out), faces)
            every_grad = every_grad.reshape(-1, width_out)
            blocks = []
            for down_step in range(3):
                for side_step in range(3):
                    window = every_pad[:, down_step : down_step + height, side_step : side_step + breadth]
                    blocks.append(
                        lax.dot_general(
                            window.reshape(-1, width_in),
                            every_grad,
                            (((0,), (0,)), ((), ())),
                            preferred_element_type=jnp.float32,
                        )
                    )
            return grad_one, jnp.concatenate(blocks, axis=0)

        def skipped(frame):
            return (
                jnp.zeros((height, breadth, width_out), jnp.bfloat16),
                jnp.zeros((9 * width_in, width_out), jnp.float32),
            )

        grad_one, total_in = lax.cond(place < tiles, rest, skipped, frame)
    else:
        grad_one = grad_hidden_of(frame)
        grad_w_in = lax.dot_general(
            unfolded_in,
            grad_one.reshape(-1, width_out),
            (((0,), (0,)), ((), ())),
            preferred_element_type=jnp.float32,
        )
        size_in = grad_w_in.shape[0]
        total = lax.psum(jnp.concatenate([grad_w_in, grad_w_out], axis=0), ("face", "tile"))
        total_in = total[:size_in]
        total_out = total[size_in:]
    squares = jnp.sum(total_in * total_in) + jnp.sum(total_out * total_out)
    factor = lax.rsqrt(squares / (total_in.size + total_out.size) + epsilon)
    update_in = (total_in * factor).astype(jnp.bfloat16)
    update_out = (total_out * factor).astype(jnp.bfloat16)
    update_in = update_in.reshape(3, 3, width_in, width_out)
    update_out = update_out.reshape(3, 3, width_out, width_out)
    return (grad_one[None, None], update_in, update_out)


def solution(mesh):
    placed = (
        P("face", "tile", None, None, None),
        P("face", "tile", None, None, None),
        P(),
        P(),
        P(),
        P(),
    )
    return jax.shard_map(
        body,
        mesh=mesh,
        in_specs=placed,
        out_specs=(P("face", "tile", None, None, None), P(), P()),
        check_vma=False,
    )
```

```python
import numpy as np
import jax
import jax.numpy as jnp
from jax import lax
from jax.sharding import PartitionSpec as P

root_half = 0.7071067811865476
inv_root_tau = 0.3989422804014327
epsilon = 1e-06
factor_budget = 48 * 2**20


def gelu_value(pre):
    return pre * 0.5 * (1.0 + lax.erf(pre * root_half))


def gelu_slope(pre):
    return 0.5 * (1.0 + lax.erf(pre * root_half)) + pre * jnp.exp(-0.5 * pre * pre) * inv_root_tau


def rim_of(cells):
    return jnp.concatenate([cells[0], cells[-1], cells[:, 0], cells[:, -1]], axis=0)


def border_of(frame):
    return jnp.concatenate([frame[0], frame[-1], frame[1:-1, 0], frame[1:-1, -1]], axis=0)


def rim_index(li, lj, height, breadth):
    return np.where(
        li == 0,
        lj,
        np.where(
            li == height - 1,
            breadth + lj,
            np.where(lj == 0, 2 * breadth + li, 2 * breadth + height + li),
        ),
    )


def face_maps(tiles, height, breadth):
    across = tiles // 4
    side = across * breadth
    rim_len = 2 * (height + breadth)
    a = np.array([0] * (breadth + 2) + [height + 1] * (breadth + 2) + list(range(1, height + 1)) * 2)
    b = np.array(list(range(breadth + 2)) * 2 + [0] * height + [breadth + 1] * height)
    t = np.arange(tiles)
    i = (t // across)[:, None] * height - 1 + a[None, :]
    j = (t % across)[:, None] * breadth - 1 + b[None, :]
    out_i = (i < 0) | (i >= side)
    out_j = (j < 0) | (j >= side)
    inside = ~out_i & ~out_j
    seam = out_i ^ out_j
    ci = np.clip(i, 0, side - 1)
    cj = np.clip(j, 0, side - 1)
    owner = (ci // height) * across + cj // breadth
    intra = np.where(inside, owner * rim_len + rim_index(ci % height, cj % breadth, height, breadth), -1)
    s = np.where(i < 0, 0, np.where(i >= side, 1, np.where(j < 0, 2, 3)))
    p = np.where(out_i, cj, ci)
    seam_cell = np.where(seam, s * side + p, -1)
    pos = np.arange(side)
    ei = np.concatenate([np.zeros(side, int), np.full(side, side - 1), pos, pos])
    ej = np.concatenate([pos, pos, np.zeros(side, int), np.full(side, side - 1)])
    sides = np.repeat(np.arange(4), side)
    li = ei % height
    lj = ej % breadth
    k = np.where(sides == 0, lj, np.where(sides == 1, breadth + lj, np.where(sides == 2, 2 * breadth + li, 2 * breadth + height + li)))
    edge = ((ei // height) * across + ej // breadth) * rim_len + k
    edge_of_rim = np.full((tiles, rim_len), -1)
    edge_of_rim[edge // rim_len, edge % rim_len] = np.arange(4 * side)
    rim_side = np.where(edge_of_rim >= 0, edge_of_rim // side, -1)
    rim_pos = np.where(edge_of_rim >= 0, edge_of_rim % side, 0)
    frame_side = np.where(seam, s, -1)
    frame_pos = np.where(seam, p, 0)
    maps = (intra, seam_cell, edge, frame_side, frame_pos, rim_side, rim_pos)
    return tuple(m.astype(np.int32) for m in maps)


def one_hot(rows, cols, dtype):
    return (rows[:, None] == cols[None, :]).astype(dtype)


def seam_source(which, pos, link_row, turn_row, side):
    link = jnp.full_like(which, -1)
    turn = jnp.zeros_like(which)
    for k in range(4):
        link = jnp.where(which == k, link_row[k], link)
        turn = jnp.where(which == k, turn_row[k], turn)
    glued = link * side + jnp.where(turn == 1, side - 1 - pos, pos)
    return jnp.where(which >= 0, glued, -1)


def halo_source(maps, place, link_row, turn_row):
    intra, _, edge, frame_side, frame_pos, _, _ = maps
    tiles, frame_len = intra.shape
    rim_len = frame_len - 4
    side = edge.shape[0] // 4
    pick = lambda table: lax.dynamic_index_in_dim(jnp.asarray(table), place, 0, False)
    glued = seam_source(pick(frame_side), pick(frame_pos), link_row, turn_row, side)
    own_intra = pick(intra)
    return jnp.where(own_intra >= 0, own_intra, jnp.where(glued >= 0, tiles * rim_len + glued, -1))


def padded_tile(cells, maps, source):
    height, breadth, depth = cells.shape
    intra, seam_cell, edge = maps[:3]
    rim_len = 2 * (height + breadth)
    tiles = intra.shape[0]
    side = edge.shape[0] // 4
    rims = lax.all_gather(rim_of(cells), "tile", axis=0, tiled=True)
    edges = jnp.dot(
        one_hot(jnp.asarray(edge), jnp.arange(tiles * rim_len), cells.dtype),
        rims,
        preferred_element_type=jnp.float32,
    ).astype(cells.dtype)
    edge_set = lax.all_gather(edges, "face", axis=0, tiled=True)
    pool = jnp.concatenate([rims, edge_set], axis=0)
    halo = jnp.dot(
        one_hot(source, jnp.arange(pool.shape[0]), cells.dtype),
        pool,
        preferred_element_type=jnp.float32,
    ).astype(cells.dtype)
    upper = halo[: breadth + 2]
    lower = halo[breadth + 2 : 2 * breadth + 4]
    left_side = halo[2 * breadth + 4 : 2 * breadth + 4 + height]
    right_side = halo[2 * breadth + 4 + height :]
    middle = jnp.concatenate([left_side[:, None], cells, right_side[:, None]], axis=1)
    return jnp.concatenate([upper[None], middle, lower[None]], axis=0)


def return_border(border, maps, place, link_row, turn_row):
    intra, seam_cell, edge, _, _, rim_side, rim_pos = maps
    tiles, frame_len = intra.shape
    rim_len = frame_len - 4
    side = edge.shape[0] // 4
    exact = lax.Precision.HIGHEST
    borders = lax.all_gather(border, "tile", axis=0, tiled=True)
    seam_sum = jnp.dot(
        one_hot(jnp.arange(4 * side), jnp.asarray(seam_cell.reshape(-1)), jnp.float32),
        borders,
        precision=exact,
    )
    seam_set = lax.all_gather(seam_sum, "face", axis=0, tiled=True)
    own_cells = place * rim_len + jnp.arange(rim_len)
    from_tiles = jnp.dot(
        one_hot(own_cells, jnp.asarray(intra.reshape(-1)), jnp.float32), borders, precision=exact
    )
    pick = lambda table: lax.dynamic_index_in_dim(jnp.asarray(table), place, 0, False)
    glued = seam_source(pick(rim_side), pick(rim_pos), link_row, turn_row, side)
    from_seams = jnp.dot(
        one_hot(glued, jnp.arange(seam_set.shape[0]), jnp.float32), seam_set, precision=exact
    )
    return from_tiles + from_seams


def unfold(padded, height, breadth):
    depth = padded.shape[2]
    windows = []
    for down_step in range(3):
        for side_step in range(3):
            windows.append(
                padded[down_step : down_step + height, side_step : side_step + breadth].reshape(
                    height * breadth, depth
                )
            )
    return jnp.concatenate(windows, axis=1)


def grad_one_size(frame):
    return (frame.shape[0] - 2) * (frame.shape[1] - 2) * frame.shape[2]


def gather_all(block, faces):
    local = lax.all_gather(block, "tile", axis=0, tiled=True)
    parts = [local]
    for shift in range(1, faces):
        pairs = [(i, (i + shift) % faces) for i in range(faces)]
        parts.append(lax.ppermute(local, "face", pairs))
    return jnp.concatenate(parts, axis=0)


def body(inputs, upstream, weight_in, weight_out, seam_link, seam_turn):
    cells = inputs[0, 0]
    height, breadth, width_in = cells.shape
    width_out = weight_out.shape[3]
    tiles = lax.axis_size("tile")
    place = lax.axis_index("tile")
    face_pos = lax.axis_index("face")
    link_row = lax.dynamic_index_in_dim(seam_link, face_pos, 0, False)
    turn_row = lax.dynamic_index_in_dim(seam_turn, face_pos, 0, False)
    maps = face_maps(tiles, height, breadth)
    source = halo_source(maps, place, link_row, turn_row)
    padded_tile_in = padded_tile(cells, maps, source)
    unfolded_in = unfold(padded_tile_in, height, breadth)
    pre_one = jnp.dot(
        unfolded_in, weight_in.reshape(-1, width_out), preferred_element_type=jnp.float32
    )
    act = gelu_value(pre_one).astype(jnp.bfloat16)
    padded_act = padded_tile(act.reshape(height, breadth, width_out), maps, source)
    unfolded_act = unfold(padded_act, height, breadth)
    kernel_out = weight_out.reshape(-1, width_out)
    pre_two = jnp.dot(unfolded_act, kernel_out, preferred_element_type=jnp.float32)
    grad_two = (upstream[0, 0].reshape(-1, width_out) * gelu_slope(pre_two)).astype(jnp.bfloat16)
    grad_w_out = lax.dot_general(
        unfolded_act, grad_two, (((0,), (0,)), ((), ())), preferred_element_type=jnp.float32
    )
    spread = lax.dot_general(
        grad_two, kernel_out, (((1,), (1,)), ((), ())), preferred_element_type=jnp.float32
    )
    frame = jnp.zeros((height + 2, breadth + 2, width_out), jnp.float32)
    for down_step in range(3):
        for side_step in range(3):
            offset = (down_step * 3 + side_step) * width_out
            piece = spread[:, offset : offset + width_out].reshape(height, breadth, width_out)
            frame = frame + jnp.pad(
                piece, ((down_step, 2 - down_step), (side_step, 2 - side_step), (0, 0))
            )
    def grad_hidden_of(frame):
        own_rim = return_border(border_of(frame), maps, place, link_row, turn_row)
        _, rim_back = jax.vjp(rim_of, jnp.zeros((height, breadth, width_out), jnp.float32))
        (rim_add,) = rim_back(own_rim)
        grad_act = frame[1:-1, 1:-1] + rim_add
        slope = gelu_slope(pre_one.reshape(height, breadth, width_out))
        return (grad_act * slope).astype(jnp.bfloat16)

    faces = lax.axis_size("face")
    gathered = faces * tiles * (padded_tile_in.size + grad_one_size(frame)) * 2
    if gathered <= factor_budget:
        total_out = lax.psum(grad_w_out, ("face", "tile"))

        def rest(frame):
            grad_one = grad_hidden_of(frame)
            every_pad = gather_all(padded_tile_in[None], faces)
            every_grad = gather_all(grad_one.reshape(1, -1, width_out), faces)
            every_grad = every_grad.reshape(-1, width_out)
            blocks = []
            for down_step in range(3):
                for side_step in range(3):
                    window = every_pad[:, down_step : down_step + height, side_step : side_step + breadth]
                    blocks.append(
                        lax.dot_general(
                            window.reshape(-1, width_in),
                            every_grad,
                            (((0,), (0,)), ((), ())),
                            preferred_element_type=jnp.float32,
                        )
                    )
            return grad_one, jnp.concatenate(blocks, axis=0)

        def skipped(frame):
            return (
                jnp.zeros((height, breadth, width_out), jnp.bfloat16),
                jnp.zeros((9 * width_in, width_out), jnp.float32),
            )

        grad_one, total_in = lax.cond(place < tiles, rest, skipped, frame)
    else:
        grad_one = grad_hidden_of(frame)
        grad_w_in = lax.dot_general(
            unfolded_in,
            grad_one.reshape(-1, width_out),
            (((0,), (0,)), ((), ())),
            preferred_element_type=jnp.float32,
        )
        size_in = grad_w_in.shape[0]
        total = lax.psum(jnp.concatenate([grad_w_in, grad_w_out], axis=0), ("face", "tile"))
        total_in = total[:size_in]
        total_out = total[size_in:]
    squares = jnp.sum(total_in * total_in) + jnp.sum(total_out * total_out)
    factor = lax.rsqrt(squares / (total_in.size + total_out.size) + epsilon)
    update_in = (total_in * factor).astype(jnp.bfloat16)
    update_out = (total_out * factor).astype(jnp.bfloat16)
    update_in = update_in.reshape(3, 3, width_in, width_out)
    update_out = update_out.reshape(3, 3, width_out, width_out)
    return (grad_one[None, None], update_in, update_out)


def solution(mesh):
    placed = (
        P("face", "tile", None, None, None),
        P("face", "tile", None, None, None),
        P(),
        P(),
        P(),
        P(),
    )
    return jax.shard_map(
        body,
        mesh=mesh,
        in_specs=placed,
        out_specs=(P("face", "tile", None, None, None), P(), P()),
        check_vma=False,
    )
```

```python
import numpy as np
import jax
import jax.numpy as jnp
from jax import lax
from jax.sharding import PartitionSpec as P

root_half = 0.7071067811865476
inv_root_tau = 0.3989422804014327
epsilon = 1e-06
factor_budget = 48 * 2**20


def gelu_value(pre):
    return pre * 0.5 * (1.0 + lax.erf(pre * root_half))


def gelu_slope(pre):
    return 0.5 * (1.0 + lax.erf(pre * root_half)) + pre * jnp.exp(-0.5 * pre * pre) * inv_root_tau


def rim_of(cells):
    return jnp.concatenate([cells[0], cells[-1], cells[:, 0], cells[:, -1]], axis=0)


def border_of(frame):
    return jnp.concatenate([frame[0], frame[-1], frame[1:-1, 0], frame[1:-1, -1]], axis=0)


def rim_index(li, lj, height, breadth):
    return np.where(
        li == 0,
        lj,
        np.where(
            li == height - 1,
            breadth + lj,
            np.where(lj == 0, 2 * breadth + li, 2 * breadth + height + li),
        ),
    )


def face_maps(tiles, height, breadth):
    across = tiles // 4
    side = across * breadth
    rim_len = 2 * (height + breadth)
    a = np.array([0] * (breadth + 2) + [height + 1] * (breadth + 2) + list(range(1, height + 1)) * 2)
    b = np.array(list(range(breadth + 2)) * 2 + [0] * height + [breadth + 1] * height)
    t = np.arange(tiles)
    i = (t // across)[:, None] * height - 1 + a[None, :]
    j = (t % across)[:, None] * breadth - 1 + b[None, :]
    out_i = (i < 0) | (i >= side)
    out_j = (j < 0) | (j >= side)
    inside = ~out_i & ~out_j
    seam = out_i ^ out_j
    ci = np.clip(i, 0, side - 1)
    cj = np.clip(j, 0, side - 1)
    owner = (ci // height) * across + cj // breadth
    intra = np.where(inside, owner * rim_len + rim_index(ci % height, cj % breadth, height, breadth), -1)
    s = np.where(i < 0, 0, np.where(i >= side, 1, np.where(j < 0, 2, 3)))
    p = np.where(out_i, cj, ci)
    seam_cell = np.where(seam, s * side + p, -1)
    pos = np.arange(side)
    ei = np.concatenate([np.zeros(side, int), np.full(side, side - 1), pos, pos])
    ej = np.concatenate([pos, pos, np.zeros(side, int), np.full(side, side - 1)])
    sides = np.repeat(np.arange(4), side)
    li = ei % height
    lj = ej % breadth
    k = np.where(sides == 0, lj, np.where(sides == 1, breadth + lj, np.where(sides == 2, 2 * breadth + li, 2 * breadth + height + li)))
    edge = ((ei // height) * across + ej // breadth) * rim_len + k
    edge_of_rim = np.full((tiles, rim_len), -1)
    edge_of_rim[edge // rim_len, edge % rim_len] = np.arange(4 * side)
    rim_side = np.where(edge_of_rim >= 0, edge_of_rim // side, -1)
    rim_pos = np.where(edge_of_rim >= 0, edge_of_rim % side, 0)
    frame_side = np.where(seam, s, -1)
    frame_pos = np.where(seam, p, 0)
    maps = (intra, seam_cell, edge, frame_side, frame_pos, rim_side, rim_pos)
    return tuple(m.astype(np.int32) for m in maps)


def one_hot(rows, cols, dtype):
    return (rows[:, None] == cols[None, :]).astype(dtype)


def seam_source(which, pos, link_row, turn_row, side):
    link = jnp.full_like(which, -1)
    turn = jnp.zeros_like(which)
    for k in range(4):
        link = jnp.where(which == k, link_row[k], link)
        turn = jnp.where(which == k, turn_row[k], turn)
    glued = link * side + jnp.where(turn == 1, side - 1 - pos, pos)
    return jnp.where(which >= 0, glued, -1)


def halo_source(maps, place, link_row, turn_row):
    intra, _, edge, frame_side, frame_pos, _, _ = maps
    tiles, frame_len = intra.shape
    rim_len = frame_len - 4
    side = edge.shape[0] // 4
    pick = lambda table: lax.dynamic_index_in_dim(jnp.asarray(table), place, 0, False)
    glued = seam_source(pick(frame_side), pick(frame_pos), link_row, turn_row, side)
    own_intra = pick(intra)
    return jnp.where(own_intra >= 0, own_intra, jnp.where(glued >= 0, tiles * rim_len + glued, -1))


def padded_tile(cells, maps, source):
    height, breadth, depth = cells.shape
    intra, seam_cell, edge = maps[:3]
    rim_len = 2 * (height + breadth)
    tiles = intra.shape[0]
    side = edge.shape[0] // 4
    rims = lax.all_gather(rim_of(cells), "tile", axis=0, tiled=True)
    edges = jnp.dot(
        one_hot(jnp.asarray(edge), jnp.arange(tiles * rim_len), cells.dtype),
        rims,
        preferred_element_type=jnp.float32,
    ).astype(cells.dtype)
    edge_set = lax.all_gather(edges, "face", axis=0, tiled=True)
    pool = jnp.concatenate([rims, edge_set], axis=0)
    halo = jnp.dot(
        one_hot(source, jnp.arange(pool.shape[0]), cells.dtype),
        pool,
        preferred_element_type=jnp.float32,
    ).astype(cells.dtype)
    upper = halo[: breadth + 2]
    lower = halo[breadth + 2 : 2 * breadth + 4]
    left_side = halo[2 * breadth + 4 : 2 * breadth + 4 + height]
    right_side = halo[2 * breadth + 4 + height :]
    middle = jnp.concatenate([left_side[:, None], cells, right_side[:, None]], axis=1)
    return jnp.concatenate([upper[None], middle, lower[None]], axis=0)


def return_border(border, maps, place, link_row, turn_row):
    intra, seam_cell, edge, _, _, rim_side, rim_pos = maps
    tiles, frame_len = intra.shape
    rim_len = frame_len - 4
    side = edge.shape[0] // 4
    exact = lax.Precision.HIGHEST
    borders = lax.all_gather(border, "tile", axis=0, tiled=True)
    seam_sum = jnp.dot(
        one_hot(jnp.arange(4 * side), jnp.asarray(seam_cell.reshape(-1)), jnp.float32),
        borders,
        precision=exact,
    )
    seam_set = lax.all_gather(seam_sum, "face", axis=0, tiled=True)
    own_cells = place * rim_len + jnp.arange(rim_len)
    from_tiles = jnp.dot(
        one_hot(own_cells, jnp.asarray(intra.reshape(-1)), jnp.float32), borders, precision=exact
    )
    pick = lambda table: lax.dynamic_index_in_dim(jnp.asarray(table), place, 0, False)
    glued = seam_source(pick(rim_side), pick(rim_pos), link_row, turn_row, side)
    from_seams = jnp.dot(
        one_hot(glued, jnp.arange(seam_set.shape[0]), jnp.float32), seam_set, precision=exact
    )
    return from_tiles + from_seams


def unfold(padded, height, breadth):
    depth = padded.shape[2]
    windows = []
    for down_step in range(3):
        for side_step in range(3):
            windows.append(
                padded[down_step : down_step + height, side_step : side_step + breadth].reshape(
                    height * breadth, depth
                )
            )
    return jnp.concatenate(windows, axis=1)


def grad_one_size(frame):
    return (frame.shape[0] - 2) * (frame.shape[1] - 2) * frame.shape[2]


def gather_all(block, faces):
    local = lax.all_gather(block, "tile", axis=0, tiled=True)
    parts = [local]
    for shift in range(1, faces):
        pairs = [(i, (i + shift) % faces) for i in range(faces)]
        parts.append(lax.ppermute(local, "face", pairs))
    return jnp.concatenate(parts, axis=0)


def body(inputs, upstream, weight_in, weight_out, seam_link, seam_turn):
    cells = inputs[0, 0]
    height, breadth, width_in = cells.shape
    width_out = weight_out.shape[3]
    tiles = lax.axis_size("tile")
    place = lax.axis_index("tile")
    face_pos = lax.axis_index("face")
    link_row = lax.dynamic_index_in_dim(seam_link, face_pos, 0, False)
    turn_row = lax.dynamic_index_in_dim(seam_turn, face_pos, 0, False)
    maps = face_maps(tiles, height, breadth)
    source = halo_source(maps, place, link_row, turn_row)
    padded_tile_in = padded_tile(cells, maps, source)
    unfolded_in = unfold(padded_tile_in, height, breadth)
    pre_one = jnp.dot(
        unfolded_in, weight_in.reshape(-1, width_out), preferred_element_type=jnp.float32
    )
    act = gelu_value(pre_one).astype(jnp.bfloat16)
    padded_act = padded_tile(act.reshape(height, breadth, width_out), maps, source)
    unfolded_act = unfold(padded_act, height, breadth)
    kernel_out = weight_out.reshape(-1, width_out)
    pre_two = jnp.dot(unfolded_act, kernel_out, preferred_element_type=jnp.float32)
    grad_two = (upstream[0, 0].reshape(-1, width_out) * gelu_slope(pre_two)).astype(jnp.bfloat16)
    grad_w_out = lax.dot_general(
        unfolded_act, grad_two, (((0,), (0,)), ((), ())), preferred_element_type=jnp.float32
    )
    spread = lax.dot_general(
        grad_two, kernel_out, (((1,), (1,)), ((), ())), preferred_element_type=jnp.float32
    )
    frame = jnp.zeros((height + 2, breadth + 2, width_out), jnp.float32)
    for down_step in range(3):
        for side_step in range(3):
            offset = (down_step * 3 + side_step) * width_out
            piece = spread[:, offset : offset + width_out].reshape(height, breadth, width_out)
            frame = frame + jnp.pad(
                piece, ((down_step, 2 - down_step), (side_step, 2 - side_step), (0, 0))
            )
    def grad_hidden_of(frame):
        own_rim = return_border(border_of(frame), maps, place, link_row, turn_row)
        _, rim_back = jax.vjp(rim_of, jnp.zeros((height, breadth, width_out), jnp.float32))
        (rim_add,) = rim_back(own_rim)
        grad_act = frame[1:-1, 1:-1] + rim_add
        slope = gelu_slope(pre_one.reshape(height, breadth, width_out))
        return (grad_act * slope).astype(jnp.bfloat16)

    faces = lax.axis_size("face")
    gathered = faces * tiles * (padded_tile_in.size + grad_one_size(frame)) * 2
    if gathered <= factor_budget:
        total_out = lax.psum(grad_w_out, ("face", "tile"))

        def rest(frame):
            grad_one = grad_hidden_of(frame)
            every_pad = gather_all(padded_tile_in[None], faces)
            every_grad = gather_all(grad_one.reshape(1, -1, width_out), faces)
            every_grad = every_grad.reshape(-1, width_out)
            def one_offset(step, blocks):
                window = lax.dynamic_slice(
                    every_pad,
                    (0, step // 3, step % 3, 0),
                    (every_pad.shape[0], height, breadth, width_in),
                )
                block = lax.dot_general(
                    window.reshape(-1, width_in),
                    every_grad,
                    (((0,), (0,)), ((), ())),
                    preferred_element_type=jnp.float32,
                )
                return lax.dynamic_update_index_in_dim(blocks, block, step, 0)

            blocks = jnp.zeros((9, width_in, width_out), jnp.float32)
            blocks = lax.fori_loop(0, 9, one_offset, blocks)
            return grad_one, blocks.reshape(9 * width_in, width_out)

        def skipped(frame):
            return (
                jnp.zeros((height, breadth, width_out), jnp.bfloat16),
                jnp.zeros((9 * width_in, width_out), jnp.float32),
            )

        grad_one, total_in = lax.cond(place < tiles, rest, skipped, frame)
    else:
        grad_one = grad_hidden_of(frame)
        grad_w_in = lax.dot_general(
            unfolded_in,
            grad_one.reshape(-1, width_out),
            (((0,), (0,)), ((), ())),
            preferred_element_type=jnp.float32,
        )
        size_in = grad_w_in.shape[0]
        total = lax.psum(jnp.concatenate([grad_w_in, grad_w_out], axis=0), ("face", "tile"))
        total_in = total[:size_in]
        total_out = total[size_in:]
    squares = jnp.sum(total_in * total_in) + jnp.sum(total_out * total_out)
    factor = lax.rsqrt(squares / (total_in.size + total_out.size) + epsilon)
    update_in = (total_in * factor).astype(jnp.bfloat16)
    update_out = (total_out * factor).astype(jnp.bfloat16)
    update_in = update_in.reshape(3, 3, width_in, width_out)
    update_out = update_out.reshape(3, 3, width_out, width_out)
    return (grad_one[None, None], update_in, update_out)


def solution(mesh):
    placed = (
        P("face", "tile", None, None, None),
        P("face", "tile", None, None, None),
        P(),
        P(),
        P(),
        P(),
    )
    return jax.shard_map(
        body,
        mesh=mesh,
        in_specs=placed,
        out_specs=(P("face", "tile", None, None, None), P(), P()),
        check_vma=False,
    )
```

```python
import numpy as np
import jax
import jax.numpy as jnp
from jax import lax
from jax.sharding import PartitionSpec as P

root_half = 0.7071067811865476
inv_root_tau = 0.3989422804014327
epsilon = 1e-06
factor_budget = 48 * 2**20


def gelu_value(pre):
    return pre * 0.5 * (1.0 + lax.erf(pre * root_half))


def gelu_slope(pre):
    return 0.5 * (1.0 + lax.erf(pre * root_half)) + pre * jnp.exp(-0.5 * pre * pre) * inv_root_tau


def rim_of(cells):
    return jnp.concatenate([cells[0], cells[-1], cells[:, 0], cells[:, -1]], axis=0)


def border_of(frame):
    return jnp.concatenate([frame[0], frame[-1], frame[1:-1, 0], frame[1:-1, -1]], axis=0)


def rim_index(li, lj, height, breadth):
    return np.where(
        li == 0,
        lj,
        np.where(
            li == height - 1,
            breadth + lj,
            np.where(lj == 0, 2 * breadth + li, 2 * breadth + height + li),
        ),
    )


def face_maps(tiles, height, breadth):
    across = tiles // 4
    side = across * breadth
    rim_len = 2 * (height + breadth)
    a = np.array([0] * (breadth + 2) + [height + 1] * (breadth + 2) + list(range(1, height + 1)) * 2)
    b = np.array(list(range(breadth + 2)) * 2 + [0] * height + [breadth + 1] * height)
    t = np.arange(tiles)
    i = (t // across)[:, None] * height - 1 + a[None, :]
    j = (t % across)[:, None] * breadth - 1 + b[None, :]
    out_i = (i < 0) | (i >= side)
    out_j = (j < 0) | (j >= side)
    inside = ~out_i & ~out_j
    seam = out_i ^ out_j
    ci = np.clip(i, 0, side - 1)
    cj = np.clip(j, 0, side - 1)
    owner = (ci // height) * across + cj // breadth
    intra = np.where(inside, owner * rim_len + rim_index(ci % height, cj % breadth, height, breadth), -1)
    s = np.where(i < 0, 0, np.where(i >= side, 1, np.where(j < 0, 2, 3)))
    p = np.where(out_i, cj, ci)
    seam_cell = np.where(seam, s * side + p, -1)
    pos = np.arange(side)
    ei = np.concatenate([np.zeros(side, int), np.full(side, side - 1), pos, pos])
    ej = np.concatenate([pos, pos, np.zeros(side, int), np.full(side, side - 1)])
    sides = np.repeat(np.arange(4), side)
    li = ei % height
    lj = ej % breadth
    k = np.where(sides == 0, lj, np.where(sides == 1, breadth + lj, np.where(sides == 2, 2 * breadth + li, 2 * breadth + height + li)))
    edge = ((ei // height) * across + ej // breadth) * rim_len + k
    edge_of_rim = np.full((tiles, rim_len), -1)
    edge_of_rim[edge // rim_len, edge % rim_len] = np.arange(4 * side)
    rim_side = np.where(edge_of_rim >= 0, edge_of_rim // side, -1)
    rim_pos = np.where(edge_of_rim >= 0, edge_of_rim % side, 0)
    frame_side = np.where(seam, s, -1)
    frame_pos = np.where(seam, p, 0)
    maps = (intra, seam_cell, edge, frame_side, frame_pos, rim_side, rim_pos)
    return tuple(m.astype(np.int32) for m in maps)


def one_hot(rows, cols, dtype):
    return (rows[:, None] == cols[None, :]).astype(dtype)


def seam_source(which, pos, link_row, turn_row, side):
    link = jnp.full_like(which, -1)
    turn = jnp.zeros_like(which)
    for k in range(4):
        link = jnp.where(which == k, link_row[k], link)
        turn = jnp.where(which == k, turn_row[k], turn)
    glued = link * side + jnp.where(turn == 1, side - 1 - pos, pos)
    return jnp.where(which >= 0, glued, -1)


def halo_source(maps, place, link_row, turn_row):
    intra, _, edge, frame_side, frame_pos, _, _ = maps
    tiles, frame_len = intra.shape
    rim_len = frame_len - 4
    side = edge.shape[0] // 4
    pick = lambda table: lax.dynamic_index_in_dim(jnp.asarray(table), place, 0, False)
    glued = seam_source(pick(frame_side), pick(frame_pos), link_row, turn_row, side)
    own_intra = pick(intra)
    return jnp.where(own_intra >= 0, own_intra, jnp.where(glued >= 0, tiles * rim_len + glued, -1))


def padded_tile(cells, maps, source):
    height, breadth, depth = cells.shape
    intra, seam_cell, edge = maps[:3]
    rim_len = 2 * (height + breadth)
    tiles = intra.shape[0]
    side = edge.shape[0] // 4
    rims = lax.all_gather(rim_of(cells), "tile", axis=0, tiled=True)
    edges = jnp.dot(
        one_hot(jnp.asarray(edge), jnp.arange(tiles * rim_len), cells.dtype),
        rims,
        preferred_element_type=jnp.float32,
    ).astype(cells.dtype)
    edge_set = lax.all_gather(edges, "face", axis=0, tiled=True)
    pool = jnp.concatenate([rims, edge_set], axis=0)
    halo = jnp.dot(
        one_hot(source, jnp.arange(pool.shape[0]), cells.dtype),
        pool,
        preferred_element_type=jnp.float32,
    ).astype(cells.dtype)
    upper = halo[: breadth + 2]
    lower = halo[breadth + 2 : 2 * breadth + 4]
    left_side = halo[2 * breadth + 4 : 2 * breadth + 4 + height]
    right_side = halo[2 * breadth + 4 + height :]
    middle = jnp.concatenate([left_side[:, None], cells, right_side[:, None]], axis=1)
    return jnp.concatenate([upper[None], middle, lower[None]], axis=0)


def return_border(border, maps, place, link_row, turn_row):
    intra, seam_cell, edge, _, _, rim_side, rim_pos = maps
    tiles, frame_len = intra.shape
    rim_len = frame_len - 4
    side = edge.shape[0] // 4
    exact = lax.Precision.HIGHEST
    borders = lax.all_gather(border, "tile", axis=0, tiled=True)
    seam_sum = jnp.dot(
        one_hot(jnp.arange(4 * side), jnp.asarray(seam_cell.reshape(-1)), jnp.float32),
        borders,
        precision=exact,
    )
    seam_set = lax.all_gather(seam_sum, "face", axis=0, tiled=True)
    own_cells = place * rim_len + jnp.arange(rim_len)
    from_tiles = jnp.dot(
        one_hot(own_cells, jnp.asarray(intra.reshape(-1)), jnp.float32), borders, precision=exact
    )
    pick = lambda table: lax.dynamic_index_in_dim(jnp.asarray(table), place, 0, False)
    glued = seam_source(pick(rim_side), pick(rim_pos), link_row, turn_row, side)
    from_seams = jnp.dot(
        one_hot(glued, jnp.arange(seam_set.shape[0]), jnp.float32), seam_set, precision=exact
    )
    return from_tiles + from_seams


def unfold(padded, height, breadth):
    depth = padded.shape[2]
    windows = []
    for down_step in range(3):
        for side_step in range(3):
            windows.append(
                padded[down_step : down_step + height, side_step : side_step + breadth].reshape(
                    height * breadth, depth
                )
            )
    return jnp.concatenate(windows, axis=1)


def grad_one_size(frame):
    return (frame.shape[0] - 2) * (frame.shape[1] - 2) * frame.shape[2]


def gather_all(block, faces):
    local = lax.all_gather(block, "tile", axis=0, tiled=True)
    parts = [local]
    for shift in range(1, faces):
        pairs = [(i, (i + shift) % faces) for i in range(faces)]
        parts.append(lax.ppermute(local, "face", pairs))
    return jnp.concatenate(parts, axis=0)


def body(inputs, upstream, weight_in, weight_out, seam_link, seam_turn):
    cells = inputs[0, 0]
    height, breadth, width_in = cells.shape
    width_out = weight_out.shape[3]
    tiles = lax.axis_size("tile")
    place = lax.axis_index("tile")
    face_pos = lax.axis_index("face")
    link_row = lax.dynamic_index_in_dim(seam_link, face_pos, 0, False)
    turn_row = lax.dynamic_index_in_dim(seam_turn, face_pos, 0, False)
    maps = face_maps(tiles, height, breadth)
    source = halo_source(maps, place, link_row, turn_row)
    padded_tile_in = padded_tile(cells, maps, source)
    unfolded_in = unfold(padded_tile_in, height, breadth)
    pre_one = jnp.dot(
        unfolded_in, weight_in.reshape(-1, width_out), preferred_element_type=jnp.float32
    )
    act = gelu_value(pre_one).astype(jnp.bfloat16)
    padded_act = padded_tile(act.reshape(height, breadth, width_out), maps, source)
    unfolded_act = unfold(padded_act, height, breadth)
    kernel_out = weight_out.reshape(-1, width_out)
    pre_two = jnp.dot(unfolded_act, kernel_out, preferred_element_type=jnp.float32)
    grad_two = (upstream[0, 0].reshape(-1, width_out) * gelu_slope(pre_two)).astype(jnp.bfloat16)
    grad_w_out = lax.dot_general(
        unfolded_act, grad_two, (((0,), (0,)), ((), ())), preferred_element_type=jnp.float32
    )
    spread = lax.dot_general(
        grad_two, kernel_out, (((1,), (1,)), ((), ())), preferred_element_type=jnp.float32
    )
    frame = jnp.zeros((height + 2, breadth + 2, width_out), jnp.float32)
    for down_step in range(3):
        for side_step in range(3):
            offset = (down_step * 3 + side_step) * width_out
            piece = spread[:, offset : offset + width_out].reshape(height, breadth, width_out)
            frame = frame + jnp.pad(
                piece, ((down_step, 2 - down_step), (side_step, 2 - side_step), (0, 0))
            )
    def grad_hidden_of(frame):
        own_rim = return_border(border_of(frame), maps, place, link_row, turn_row)
        _, rim_back = jax.vjp(rim_of, jnp.zeros((height, breadth, width_out), jnp.float32))
        (rim_add,) = rim_back(own_rim)
        grad_act = frame[1:-1, 1:-1] + rim_add
        slope = gelu_slope(pre_one.reshape(height, breadth, width_out))
        return (grad_act * slope).astype(jnp.bfloat16)

    faces = lax.axis_size("face")
    gathered = faces * tiles * (padded_tile_in.size + grad_one_size(frame)) * 2
    if gathered <= factor_budget:
        total_out = lax.psum(grad_w_out, ("face", "tile"))

        def rest(frame):
            grad_one = grad_hidden_of(frame)
            every_pad = gather_all(padded_tile_in[None], faces)
            every_grad = gather_all(grad_one.reshape(1, -1, width_out), faces)
            every_grad = every_grad.reshape(-1, width_out)
            windows = jnp.concatenate(
                [
                    every_pad[:, down_step : down_step + height, side_step : side_step + breadth].reshape(
                        -1, width_in
                    )
                    for down_step in range(3)
                    for side_step in range(3)
                ],
                axis=1,
            )
            total_in = lax.dot_general(
                windows, every_grad, (((0,), (0,)), ((), ())), preferred_element_type=jnp.float32
            )
            return grad_one, total_in

        def skipped(frame):
            return (
                jnp.zeros((height, breadth, width_out), jnp.bfloat16),
                jnp.zeros((9 * width_in, width_out), jnp.float32),
            )

        grad_one, total_in = lax.cond(place < tiles, rest, skipped, frame)
    else:
        grad_one = grad_hidden_of(frame)
        grad_w_in = lax.dot_general(
            unfolded_in,
            grad_one.reshape(-1, width_out),
            (((0,), (0,)), ((), ())),
            preferred_element_type=jnp.float32,
        )
        size_in = grad_w_in.shape[0]
        total = lax.psum(jnp.concatenate([grad_w_in, grad_w_out], axis=0), ("face", "tile"))
        total_in = total[:size_in]
        total_out = total[size_in:]
    squares = jnp.sum(total_in * total_in) + jnp.sum(total_out * total_out)
    factor = lax.rsqrt(squares / (total_in.size + total_out.size) + epsilon)
    update_in = (total_in * factor).astype(jnp.bfloat16)
    update_out = (total_out * factor).astype(jnp.bfloat16)
    update_in = update_in.reshape(3, 3, width_in, width_out)
    update_out = update_out.reshape(3, 3, width_out, width_out)
    return (grad_one[None, None], update_in, update_out)


def solution(mesh):
    placed = (
        P("face", "tile", None, None, None),
        P("face", "tile", None, None, None),
        P(),
        P(),
        P(),
        P(),
    )
    return jax.shard_map(
        body,
        mesh=mesh,
        in_specs=placed,
        out_specs=(P("face", "tile", None, None, None), P(), P()),
        check_vma=False,
    )
```

```python
import numpy as np
import jax
import jax.numpy as jnp
from jax import lax
from jax.sharding import PartitionSpec as P

root_half = 0.7071067811865476
inv_root_tau = 0.3989422804014327
epsilon = 1e-06
factor_budget = 48 * 2**20


def gelu_value(pre):
    return pre * 0.5 * (1.0 + lax.erf(pre * root_half))


def gelu_slope(pre):
    return 0.5 * (1.0 + lax.erf(pre * root_half)) + pre * jnp.exp(-0.5 * pre * pre) * inv_root_tau


def rim_of(cells):
    return jnp.concatenate([cells[0], cells[-1], cells[:, 0], cells[:, -1]], axis=0)


def border_of(frame):
    return jnp.concatenate([frame[0], frame[-1], frame[1:-1, 0], frame[1:-1, -1]], axis=0)


def rim_index(li, lj, height, breadth):
    return np.where(
        li == 0,
        lj,
        np.where(
            li == height - 1,
            breadth + lj,
            np.where(lj == 0, 2 * breadth + li, 2 * breadth + height + li),
        ),
    )


def face_maps(tiles, height, breadth):
    across = tiles // 4
    side = across * breadth
    rim_len = 2 * (height + breadth)
    a = np.array([0] * (breadth + 2) + [height + 1] * (breadth + 2) + list(range(1, height + 1)) * 2)
    b = np.array(list(range(breadth + 2)) * 2 + [0] * height + [breadth + 1] * height)
    t = np.arange(tiles)
    i = (t // across)[:, None] * height - 1 + a[None, :]
    j = (t % across)[:, None] * breadth - 1 + b[None, :]
    out_i = (i < 0) | (i >= side)
    out_j = (j < 0) | (j >= side)
    inside = ~out_i & ~out_j
    seam = out_i ^ out_j
    ci = np.clip(i, 0, side - 1)
    cj = np.clip(j, 0, side - 1)
    owner = (ci // height) * across + cj // breadth
    intra = np.where(inside, owner * rim_len + rim_index(ci % height, cj % breadth, height, breadth), -1)
    s = np.where(i < 0, 0, np.where(i >= side, 1, np.where(j < 0, 2, 3)))
    p = np.where(out_i, cj, ci)
    seam_cell = np.where(seam, s * side + p, -1)
    pos = np.arange(side)
    ei = np.concatenate([np.zeros(side, int), np.full(side, side - 1), pos, pos])
    ej = np.concatenate([pos, pos, np.zeros(side, int), np.full(side, side - 1)])
    sides = np.repeat(np.arange(4), side)
    li = ei % height
    lj = ej % breadth
    k = np.where(sides == 0, lj, np.where(sides == 1, breadth + lj, np.where(sides == 2, 2 * breadth + li, 2 * breadth + height + li)))
    edge = ((ei // height) * across + ej // breadth) * rim_len + k
    edge_of_rim = np.full((tiles, rim_len), -1)
    edge_of_rim[edge // rim_len, edge % rim_len] = np.arange(4 * side)
    rim_side = np.where(edge_of_rim >= 0, edge_of_rim // side, -1)
    rim_pos = np.where(edge_of_rim >= 0, edge_of_rim % side, 0)
    frame_side = np.where(seam, s, -1)
    frame_pos = np.where(seam, p, 0)
    maps = (intra, seam_cell, edge, frame_side, frame_pos, rim_side, rim_pos)
    return tuple(m.astype(np.int32) for m in maps)


def one_hot(rows, cols, dtype):
    return (rows[:, None] == cols[None, :]).astype(dtype)


def seam_source(which, pos, link_row, turn_row, side):
    hit = which[:, None] == jnp.arange(4, dtype=which.dtype)[None, :]
    link = jnp.sum(jnp.where(hit, link_row[None, :], 0), axis=1)
    turn = jnp.sum(jnp.where(hit, turn_row[None, :], 0), axis=1)
    glued = link * side + jnp.where(turn == 1, side - 1 - pos, pos)
    return jnp.where(which >= 0, glued, -1)


def halo_source(maps, place, link_row, turn_row):
    intra, _, edge, frame_side, frame_pos, _, _ = maps
    tiles, frame_len = intra.shape
    rim_len = frame_len - 4
    side = edge.shape[0] // 4
    pick = lambda table: lax.dynamic_index_in_dim(jnp.asarray(table), place, 0, False)
    glued = seam_source(pick(frame_side), pick(frame_pos), link_row, turn_row, side)
    own_intra = pick(intra)
    return jnp.where(own_intra >= 0, own_intra, jnp.where(glued >= 0, tiles * rim_len + glued, -1))


def padded_tile(cells, maps, source):
    height, breadth, depth = cells.shape
    intra, seam_cell, edge = maps[:3]
    rim_len = 2 * (height + breadth)
    tiles = intra.shape[0]
    side = edge.shape[0] // 4
    rims = lax.all_gather(rim_of(cells), "tile", axis=0, tiled=True)
    edges = jnp.dot(
        one_hot(jnp.asarray(edge), jnp.arange(tiles * rim_len), cells.dtype),
        rims,
        preferred_element_type=jnp.float32,
    ).astype(cells.dtype)
    edge_set = lax.all_gather(edges, "face", axis=0, tiled=True)
    pool = jnp.concatenate([rims, edge_set], axis=0)
    halo = jnp.dot(
        one_hot(source, jnp.arange(pool.shape[0]), cells.dtype),
        pool,
        preferred_element_type=jnp.float32,
    ).astype(cells.dtype)
    upper = halo[: breadth + 2]
    lower = halo[breadth + 2 : 2 * breadth + 4]
    left_side = halo[2 * breadth + 4 : 2 * breadth + 4 + height]
    right_side = halo[2 * breadth + 4 + height :]
    middle = jnp.concatenate([left_side[:, None], cells, right_side[:, None]], axis=1)
    return jnp.concatenate([upper[None], middle, lower[None]], axis=0)


def return_border(border, maps, place, link_row, turn_row):
    intra, seam_cell, edge, _, _, rim_side, rim_pos = maps
    tiles, frame_len = intra.shape
    rim_len = frame_len - 4
    side = edge.shape[0] // 4
    exact = lax.Precision.HIGHEST
    borders = lax.all_gather(border, "tile", axis=0, tiled=True)
    seam_sum = jnp.dot(
        one_hot(jnp.arange(4 * side), jnp.asarray(seam_cell.reshape(-1)), jnp.float32),
        borders,
        precision=exact,
    )
    seam_set = lax.all_gather(seam_sum, "face", axis=0, tiled=True)
    own_cells = place * rim_len + jnp.arange(rim_len)
    from_tiles = jnp.dot(
        one_hot(own_cells, jnp.asarray(intra.reshape(-1)), jnp.float32), borders, precision=exact
    )
    pick = lambda table: lax.dynamic_index_in_dim(jnp.asarray(table), place, 0, False)
    glued = seam_source(pick(rim_side), pick(rim_pos), link_row, turn_row, side)
    from_seams = jnp.dot(
        one_hot(glued, jnp.arange(seam_set.shape[0]), jnp.float32), seam_set, precision=exact
    )
    return from_tiles + from_seams


def unfold(padded, height, breadth):
    depth = padded.shape[2]
    windows = []
    for down_step in range(3):
        for side_step in range(3):
            windows.append(
                padded[down_step : down_step + height, side_step : side_step + breadth].reshape(
                    height * breadth, depth
                )
            )
    return jnp.concatenate(windows, axis=1)


def grad_one_size(frame):
    return (frame.shape[0] - 2) * (frame.shape[1] - 2) * frame.shape[2]


def gather_all(block, faces):
    local = lax.all_gather(block, "tile", axis=0, tiled=True)
    parts = [local]
    for shift in range(1, faces):
        pairs = [(i, (i + shift) % faces) for i in range(faces)]
        parts.append(lax.ppermute(local, "face", pairs))
    return jnp.concatenate(parts, axis=0)


def body(inputs, upstream, weight_in, weight_out, seam_link, seam_turn):
    cells = inputs[0, 0]
    height, breadth, width_in = cells.shape
    width_out = weight_out.shape[3]
    tiles = lax.axis_size("tile")
    place = lax.axis_index("tile")
    face_pos = lax.axis_index("face")
    link_row = lax.dynamic_index_in_dim(seam_link, face_pos, 0, False)
    turn_row = lax.dynamic_index_in_dim(seam_turn, face_pos, 0, False)
    maps = face_maps(tiles, height, breadth)
    source = halo_source(maps, place, link_row, turn_row)
    padded_tile_in = padded_tile(cells, maps, source)
    unfolded_in = unfold(padded_tile_in, height, breadth)
    pre_one = jnp.dot(
        unfolded_in, weight_in.reshape(-1, width_out), preferred_element_type=jnp.float32
    )
    act = gelu_value(pre_one).astype(jnp.bfloat16)
    padded_act = padded_tile(act.reshape(height, breadth, width_out), maps, source)
    unfolded_act = unfold(padded_act, height, breadth)
    kernel_out = weight_out.reshape(-1, width_out)
    pre_two = jnp.dot(unfolded_act, kernel_out, preferred_element_type=jnp.float32)
    grad_two = (upstream[0, 0].reshape(-1, width_out) * gelu_slope(pre_two)).astype(jnp.bfloat16)
    grad_w_out = lax.dot_general(
        unfolded_act, grad_two, (((0,), (0,)), ((), ())), preferred_element_type=jnp.float32
    )
    spread = lax.dot_general(
        grad_two, kernel_out, (((1,), (1,)), ((), ())), preferred_element_type=jnp.float32
    )
    frame = jnp.zeros((height + 2, breadth + 2, width_out), jnp.float32)
    for down_step in range(3):
        for side_step in range(3):
            offset = (down_step * 3 + side_step) * width_out
            piece = spread[:, offset : offset + width_out].reshape(height, breadth, width_out)
            frame = frame + jnp.pad(
                piece, ((down_step, 2 - down_step), (side_step, 2 - side_step), (0, 0))
            )
    def grad_hidden_of(frame):
        own_rim = return_border(border_of(frame), maps, place, link_row, turn_row)
        _, rim_back = jax.vjp(rim_of, jnp.zeros((height, breadth, width_out), jnp.float32))
        (rim_add,) = rim_back(own_rim)
        grad_act = frame[1:-1, 1:-1] + rim_add
        slope = gelu_slope(pre_one.reshape(height, breadth, width_out))
        return (grad_act * slope).astype(jnp.bfloat16)

    faces = lax.axis_size("face")
    gathered = faces * tiles * (padded_tile_in.size + grad_one_size(frame)) * 2
    if gathered <= factor_budget:
        total_out = lax.psum(grad_w_out, ("face", "tile"))

        def rest(frame):
            grad_one = grad_hidden_of(frame)
            every_pad = gather_all(padded_tile_in[None], faces)
            every_grad = gather_all(grad_one.reshape(1, -1, width_out), faces)
            every_grad = every_grad.reshape(-1, width_out)
            blocks = []
            for down_step in range(3):
                for side_step in range(3):
                    window = every_pad[:, down_step : down_step + height, side_step : side_step + breadth]
                    blocks.append(
                        lax.dot_general(
                            window.reshape(-1, width_in),
                            every_grad,
                            (((0,), (0,)), ((), ())),
                            preferred_element_type=jnp.float32,
                        )
                    )
            return grad_one, jnp.concatenate(blocks, axis=0)

        def skipped(frame):
            return (
                jnp.zeros((height, breadth, width_out), jnp.bfloat16),
                jnp.zeros((9 * width_in, width_out), jnp.float32),
            )

        grad_one, total_in = lax.cond(place < tiles, rest, skipped, frame)
    else:
        grad_one = grad_hidden_of(frame)
        grad_w_in = lax.dot_general(
            unfolded_in,
            grad_one.reshape(-1, width_out),
            (((0,), (0,)), ((), ())),
            preferred_element_type=jnp.float32,
        )
        size_in = grad_w_in.shape[0]
        total = lax.psum(jnp.concatenate([grad_w_in, grad_w_out], axis=0), ("face", "tile"))
        total_in = total[:size_in]
        total_out = total[size_in:]
    squares = jnp.sum(total_in * total_in) + jnp.sum(total_out * total_out)
    factor = lax.rsqrt(squares / (total_in.size + total_out.size) + epsilon)
    update_in = (total_in * factor).astype(jnp.bfloat16)
    update_out = (total_out * factor).astype(jnp.bfloat16)
    update_in = update_in.reshape(3, 3, width_in, width_out)
    update_out = update_out.reshape(3, 3, width_out, width_out)
    return (grad_one[None, None], update_in, update_out)


def solution(mesh):
    placed = (
        P("face", "tile", None, None, None),
        P("face", "tile", None, None, None),
        P(),
        P(),
        P(),
        P(),
    )
    return jax.shard_map(
        body,
        mesh=mesh,
        in_specs=placed,
        out_specs=(P("face", "tile", None, None, None), P(), P()),
        check_vma=False,
    )
```

```python
import numpy as np
import jax
import jax.numpy as jnp
from jax import lax
from jax.sharding import PartitionSpec as P

root_half = 0.7071067811865476
inv_root_tau = 0.3989422804014327
epsilon = 1e-06
factor_budget = 48 * 2**20


def gelu_value(pre):
    return pre * 0.5 * (1.0 + lax.erf(pre * root_half))


def gelu_slope(pre):
    return 0.5 * (1.0 + lax.erf(pre * root_half)) + pre * jnp.exp(-0.5 * pre * pre) * inv_root_tau


def rim_of(cells):
    return jnp.concatenate([cells[0], cells[-1], cells[:, 0], cells[:, -1]], axis=0)


def border_of(frame):
    return jnp.concatenate([frame[0], frame[-1], frame[1:-1, 0], frame[1:-1, -1]], axis=0)


def rim_index(li, lj, height, breadth):
    return np.where(
        li == 0,
        lj,
        np.where(
            li == height - 1,
            breadth + lj,
            np.where(lj == 0, 2 * breadth + li, 2 * breadth + height + li),
        ),
    )


def face_maps(tiles, height, breadth):
    across = tiles // 4
    side = across * breadth
    rim_len = 2 * (height + breadth)
    a = np.array([0] * (breadth + 2) + [height + 1] * (breadth + 2) + list(range(1, height + 1)) * 2)
    b = np.array(list(range(breadth + 2)) * 2 + [0] * height + [breadth + 1] * height)
    t = np.arange(tiles)
    i = (t // across)[:, None] * height - 1 + a[None, :]
    j = (t % across)[:, None] * breadth - 1 + b[None, :]
    out_i = (i < 0) | (i >= side)
    out_j = (j < 0) | (j >= side)
    inside = ~out_i & ~out_j
    seam = out_i ^ out_j
    ci = np.clip(i, 0, side - 1)
    cj = np.clip(j, 0, side - 1)
    owner = (ci // height) * across + cj // breadth
    intra = np.where(inside, owner * rim_len + rim_index(ci % height, cj % breadth, height, breadth), -1)
    s = np.where(i < 0, 0, np.where(i >= side, 1, np.where(j < 0, 2, 3)))
    p = np.where(out_i, cj, ci)
    seam_cell = np.where(seam, s * side + p, -1)
    pos = np.arange(side)
    ei = np.concatenate([np.zeros(side, int), np.full(side, side - 1), pos, pos])
    ej = np.concatenate([pos, pos, np.zeros(side, int), np.full(side, side - 1)])
    sides = np.repeat(np.arange(4), side)
    li = ei % height
    lj = ej % breadth
    k = np.where(sides == 0, lj, np.where(sides == 1, breadth + lj, np.where(sides == 2, 2 * breadth + li, 2 * breadth + height + li)))
    edge = ((ei // height) * across + ej // breadth) * rim_len + k
    edge_of_rim = np.full((tiles, rim_len), -1)
    edge_of_rim[edge // rim_len, edge % rim_len] = np.arange(4 * side)
    rim_side = np.where(edge_of_rim >= 0, edge_of_rim // side, -1)
    rim_pos = np.where(edge_of_rim >= 0, edge_of_rim % side, 0)
    frame_side = np.where(seam, s, -1)
    frame_pos = np.where(seam, p, 0)
    maps = (intra, seam_cell, edge, frame_side, frame_pos, rim_side, rim_pos)
    return tuple(m.astype(np.int32) for m in maps)


def one_hot(rows, cols, dtype):
    return (rows[:, None] == cols[None, :]).astype(dtype)


def seam_source(which, pos, link_row, turn_row, side):
    hit = which[:, None] == jnp.arange(4, dtype=which.dtype)[None, :]
    link = jnp.sum(jnp.where(hit, link_row[None, :], 0), axis=1)
    turn = jnp.sum(jnp.where(hit, turn_row[None, :], 0), axis=1)
    glued = link * side + jnp.where(turn == 1, side - 1 - pos, pos)
    return jnp.where(which >= 0, glued, -1)


def halo_source(maps, place, link_row, turn_row):
    intra, _, edge, frame_side, frame_pos, _, _ = maps
    tiles, frame_len = intra.shape
    rim_len = frame_len - 4
    side = edge.shape[0] // 4
    pick = lambda table: lax.dynamic_index_in_dim(jnp.asarray(table), place, 0, False)
    glued = seam_source(pick(frame_side), pick(frame_pos), link_row, turn_row, side)
    own_intra = pick(intra)
    return jnp.where(own_intra >= 0, own_intra, jnp.where(glued >= 0, tiles * rim_len + glued, -1))


def padded_tile(cells, maps, source):
    height, breadth, depth = cells.shape
    intra, seam_cell, edge = maps[:3]
    rim_len = 2 * (height + breadth)
    tiles = intra.shape[0]
    side = edge.shape[0] // 4
    rims = lax.all_gather(rim_of(cells), "tile", axis=0, tiled=True)
    edges = jnp.dot(
        one_hot(jnp.asarray(edge), jnp.arange(tiles * rim_len), cells.dtype),
        rims,
        preferred_element_type=jnp.float32,
    ).astype(cells.dtype)
    faces = lax.axis_size("face")
    parts = [edges]
    for shift in range(1, faces):
        pairs = [(i, (i + shift) % faces) for i in range(faces)]
        parts.append(lax.ppermute(edges, "face", pairs))
    pool = jnp.concatenate([rims] + parts, axis=0)
    halo = jnp.dot(
        one_hot(source, jnp.arange(pool.shape[0]), cells.dtype),
        pool,
        preferred_element_type=jnp.float32,
    ).astype(cells.dtype)
    upper = halo[: breadth + 2]
    lower = halo[breadth + 2 : 2 * breadth + 4]
    left_side = halo[2 * breadth + 4 : 2 * breadth + 4 + height]
    right_side = halo[2 * breadth + 4 + height :]
    middle = jnp.concatenate([left_side[:, None], cells, right_side[:, None]], axis=1)
    return jnp.concatenate([upper[None], middle, lower[None]], axis=0)


def return_border(border, maps, place, link_row, turn_row):
    intra, seam_cell, edge, _, _, rim_side, rim_pos = maps
    tiles, frame_len = intra.shape
    rim_len = frame_len - 4
    side = edge.shape[0] // 4
    exact = lax.Precision.HIGHEST
    borders = lax.all_gather(border, "tile", axis=0, tiled=True)
    seam_sum = jnp.dot(
        one_hot(jnp.arange(4 * side), jnp.asarray(seam_cell.reshape(-1)), jnp.float32),
        borders,
        precision=exact,
    )
    seam_set = lax.all_gather(seam_sum, "face", axis=0, tiled=True)
    own_cells = place * rim_len + jnp.arange(rim_len)
    from_tiles = jnp.dot(
        one_hot(own_cells, jnp.asarray(intra.reshape(-1)), jnp.float32), borders, precision=exact
    )
    pick = lambda table: lax.dynamic_index_in_dim(jnp.asarray(table), place, 0, False)
    glued = seam_source(pick(rim_side), pick(rim_pos), link_row, turn_row, side)
    from_seams = jnp.dot(
        one_hot(glued, jnp.arange(seam_set.shape[0]), jnp.float32), seam_set, precision=exact
    )
    return from_tiles + from_seams


def unfold(padded, height, breadth):
    depth = padded.shape[2]
    windows = []
    for down_step in range(3):
        for side_step in range(3):
            windows.append(
                padded[down_step : down_step + height, side_step : side_step + breadth].reshape(
                    height * breadth, depth
                )
            )
    return jnp.concatenate(windows, axis=1)


def grad_one_size(frame):
    return (frame.shape[0] - 2) * (frame.shape[1] - 2) * frame.shape[2]


def gather_all(block, faces):
    local = lax.all_gather(block, "tile", axis=0, tiled=True)
    parts = [local]
    for shift in range(1, faces):
        pairs = [(i, (i + shift) % faces) for i in range(faces)]
        parts.append(lax.ppermute(local, "face", pairs))
    return jnp.concatenate(parts, axis=0)


def body(inputs, upstream, weight_in, weight_out, seam_link, seam_turn):
    cells = inputs[0, 0]
    height, breadth, width_in = cells.shape
    width_out = weight_out.shape[3]
    tiles = lax.axis_size("tile")
    place = lax.axis_index("tile")
    face_pos = lax.axis_index("face")
    link_row = lax.dynamic_index_in_dim(seam_link, face_pos, 0, False)
    turn_row = lax.dynamic_index_in_dim(seam_turn, face_pos, 0, False)
    maps = face_maps(tiles, height, breadth)
    faces = lax.axis_size("face")
    offset_row = ((face_pos - link_row // 4) % faces) * 4 + link_row % 4
    source = halo_source(maps, place, offset_row, turn_row)
    padded_tile_in = padded_tile(cells, maps, source)
    unfolded_in = unfold(padded_tile_in, height, breadth)
    pre_one = jnp.dot(
        unfolded_in, weight_in.reshape(-1, width_out), preferred_element_type=jnp.float32
    )
    act = gelu_value(pre_one).astype(jnp.bfloat16)
    padded_act = padded_tile(act.reshape(height, breadth, width_out), maps, source)
    unfolded_act = unfold(padded_act, height, breadth)
    kernel_out = weight_out.reshape(-1, width_out)
    pre_two = jnp.dot(unfolded_act, kernel_out, preferred_element_type=jnp.float32)
    grad_two = (upstream[0, 0].reshape(-1, width_out) * gelu_slope(pre_two)).astype(jnp.bfloat16)
    grad_w_out = lax.dot_general(
        unfolded_act, grad_two, (((0,), (0,)), ((), ())), preferred_element_type=jnp.float32
    )
    spread = lax.dot_general(
        grad_two, kernel_out, (((1,), (1,)), ((), ())), preferred_element_type=jnp.float32
    )
    frame = jnp.zeros((height + 2, breadth + 2, width_out), jnp.float32)
    for down_step in range(3):
        for side_step in range(3):
            offset = (down_step * 3 + side_step) * width_out
            piece = spread[:, offset : offset + width_out].reshape(height, breadth, width_out)
            frame = frame + jnp.pad(
                piece, ((down_step, 2 - down_step), (side_step, 2 - side_step), (0, 0))
            )
    def grad_hidden_of(frame):
        own_rim = return_border(border_of(frame), maps, place, link_row, turn_row)
        _, rim_back = jax.vjp(rim_of, jnp.zeros((height, breadth, width_out), jnp.float32))
        (rim_add,) = rim_back(own_rim)
        grad_act = frame[1:-1, 1:-1] + rim_add
        slope = gelu_slope(pre_one.reshape(height, breadth, width_out))
        return (grad_act * slope).astype(jnp.bfloat16)

    faces = lax.axis_size("face")
    gathered = faces * tiles * (padded_tile_in.size + grad_one_size(frame)) * 2
    if gathered <= factor_budget:
        total_out = lax.psum(grad_w_out, ("face", "tile"))

        def rest(frame):
            grad_one = grad_hidden_of(frame)
            every_pad = gather_all(padded_tile_in[None], faces)
            every_grad = gather_all(grad_one.reshape(1, -1, width_out), faces)
            every_grad = every_grad.reshape(-1, width_out)
            blocks = []
            for down_step in range(3):
                for side_step in range(3):
                    window = every_pad[:, down_step : down_step + height, side_step : side_step + breadth]
                    blocks.append(
                        lax.dot_general(
                            window.reshape(-1, width_in),
                            every_grad,
                            (((0,), (0,)), ((), ())),
                            preferred_element_type=jnp.float32,
                        )
                    )
            return grad_one, jnp.concatenate(blocks, axis=0)

        def skipped(frame):
            return (
                jnp.zeros((height, breadth, width_out), jnp.bfloat16),
                jnp.zeros((9 * width_in, width_out), jnp.float32),
            )

        grad_one, total_in = lax.cond(place < tiles, rest, skipped, frame)
    else:
        grad_one = grad_hidden_of(frame)
        grad_w_in = lax.dot_general(
            unfolded_in,
            grad_one.reshape(-1, width_out),
            (((0,), (0,)), ((), ())),
            preferred_element_type=jnp.float32,
        )
        size_in = grad_w_in.shape[0]
        total = lax.psum(jnp.concatenate([grad_w_in, grad_w_out], axis=0), ("face", "tile"))
        total_in = total[:size_in]
        total_out = total[size_in:]
    squares = jnp.sum(total_in * total_in) + jnp.sum(total_out * total_out)
    factor = lax.rsqrt(squares / (total_in.size + total_out.size) + epsilon)
    update_in = (total_in * factor).astype(jnp.bfloat16)
    update_out = (total_out * factor).astype(jnp.bfloat16)
    update_in = update_in.reshape(3, 3, width_in, width_out)
    update_out = update_out.reshape(3, 3, width_out, width_out)
    return (grad_one[None, None], update_in, update_out)


def solution(mesh):
    placed = (
        P("face", "tile", None, None, None),
        P("face", "tile", None, None, None),
        P(),
        P(),
        P(),
        P(),
    )
    return jax.shard_map(
        body,
        mesh=mesh,
        in_specs=placed,
        out_specs=(P("face", "tile", None, None, None), P(), P()),
        check_vma=False,
    )
```

```python
import numpy as np
import jax
import jax.numpy as jnp
from jax import lax
from jax.sharding import PartitionSpec as P
from jax.experimental import pallas as pl

root_half = 0.7071067811865476
inv_root_tau = 0.3989422804014327
epsilon = 1e-06
factor_budget = 48 * 2**20


def scale_kernel(in_ref, out_ref, update_in_ref, update_out_ref):
    grad_in = in_ref[...]
    grad_out = out_ref[...]
    squares = jnp.sum(grad_in * grad_in, axis=(0, 1), keepdims=True) + jnp.sum(
        grad_out * grad_out, axis=(0, 1), keepdims=True
    )
    factor = lax.rsqrt(squares / (grad_in.size + grad_out.size) + epsilon)
    update_in_ref[...] = (grad_in * factor).astype(update_in_ref.dtype)
    update_out_ref[...] = (grad_out * factor).astype(update_out_ref.dtype)


def gelu_value(pre):
    return pre * 0.5 * (1.0 + lax.erf(pre * root_half))


def gelu_slope(pre):
    return 0.5 * (1.0 + lax.erf(pre * root_half)) + pre * jnp.exp(-0.5 * pre * pre) * inv_root_tau


def rim_of(cells):
    return jnp.concatenate([cells[0], cells[-1], cells[:, 0], cells[:, -1]], axis=0)


def border_of(frame):
    return jnp.concatenate([frame[0], frame[-1], frame[1:-1, 0], frame[1:-1, -1]], axis=0)


def rim_index(li, lj, height, breadth):
    return np.where(
        li == 0,
        lj,
        np.where(
            li == height - 1,
            breadth + lj,
            np.where(lj == 0, 2 * breadth + li, 2 * breadth + height + li),
        ),
    )


def face_maps(tiles, height, breadth):
    across = tiles // 4
    side = across * breadth
    rim_len = 2 * (height + breadth)
    a = np.array([0] * (breadth + 2) + [height + 1] * (breadth + 2) + list(range(1, height + 1)) * 2)
    b = np.array(list(range(breadth + 2)) * 2 + [0] * height + [breadth + 1] * height)
    t = np.arange(tiles)
    i = (t // across)[:, None] * height - 1 + a[None, :]
    j = (t % across)[:, None] * breadth - 1 + b[None, :]
    out_i = (i < 0) | (i >= side)
    out_j = (j < 0) | (j >= side)
    inside = ~out_i & ~out_j
    seam = out_i ^ out_j
    ci = np.clip(i, 0, side - 1)
    cj = np.clip(j, 0, side - 1)
    owner = (ci // height) * across + cj // breadth
    intra = np.where(inside, owner * rim_len + rim_index(ci % height, cj % breadth, height, breadth), -1)
    s = np.where(i < 0, 0, np.where(i >= side, 1, np.where(j < 0, 2, 3)))
    p = np.where(out_i, cj, ci)
    seam_cell = np.where(seam, s * side + p, -1)
    pos = np.arange(side)
    ei = np.concatenate([np.zeros(side, int), np.full(side, side - 1), pos, pos])
    ej = np.concatenate([pos, pos, np.zeros(side, int), np.full(side, side - 1)])
    sides = np.repeat(np.arange(4), side)
    li = ei % height
    lj = ej % breadth
    k = np.where(sides == 0, lj, np.where(sides == 1, breadth + lj, np.where(sides == 2, 2 * breadth + li, 2 * breadth + height + li)))
    edge = ((ei // height) * across + ej // breadth) * rim_len + k
    edge_of_rim = np.full((tiles, rim_len), -1)
    edge_of_rim[edge // rim_len, edge % rim_len] = np.arange(4 * side)
    rim_side = np.where(edge_of_rim >= 0, edge_of_rim // side, -1)
    rim_pos = np.where(edge_of_rim >= 0, edge_of_rim % side, 0)
    frame_side = np.where(seam, s, -1)
    frame_pos = np.where(seam, p, 0)
    maps = (intra, seam_cell, edge, frame_side, frame_pos, rim_side, rim_pos)
    return tuple(m.astype(np.int32) for m in maps)


def one_hot(rows, cols, dtype):
    return (rows[:, None] == cols[None, :]).astype(dtype)


def seam_source(which, pos, link_row, turn_row, side):
    hit = which[:, None] == jnp.arange(4, dtype=which.dtype)[None, :]
    link = jnp.sum(jnp.where(hit, link_row[None, :], 0), axis=1)
    turn = jnp.sum(jnp.where(hit, turn_row[None, :], 0), axis=1)
    glued = link * side + jnp.where(turn == 1, side - 1 - pos, pos)
    return jnp.where(which >= 0, glued, -1)


def halo_source(maps, place, link_row, turn_row):
    intra, _, edge, frame_side, frame_pos, _, _ = maps
    tiles, frame_len = intra.shape
    rim_len = frame_len - 4
    side = edge.shape[0] // 4
    pick = lambda table: lax.dynamic_index_in_dim(jnp.asarray(table), place, 0, False)
    glued = seam_source(pick(frame_side), pick(frame_pos), link_row, turn_row, side)
    own_intra = pick(intra)
    return jnp.where(own_intra >= 0, own_intra, jnp.where(glued >= 0, tiles * rim_len + glued, -1))


def padded_tile(cells, maps, source):
    height, breadth, depth = cells.shape
    intra, seam_cell, edge = maps[:3]
    rim_len = 2 * (height + breadth)
    tiles = intra.shape[0]
    side = edge.shape[0] // 4
    rims = lax.all_gather(rim_of(cells), "tile", axis=0, tiled=True)
    edges = jnp.dot(
        one_hot(jnp.asarray(edge), jnp.arange(tiles * rim_len), cells.dtype),
        rims,
        preferred_element_type=jnp.float32,
    ).astype(cells.dtype)
    edge_set = lax.all_gather(edges, "face", axis=0, tiled=True)
    pool = jnp.concatenate([rims, edge_set], axis=0)
    halo = jnp.dot(
        one_hot(source, jnp.arange(pool.shape[0]), cells.dtype),
        pool,
        preferred_element_type=jnp.float32,
    ).astype(cells.dtype)
    upper = halo[: breadth + 2]
    lower = halo[breadth + 2 : 2 * breadth + 4]
    left_side = halo[2 * breadth + 4 : 2 * breadth + 4 + height]
    right_side = halo[2 * breadth + 4 + height :]
    middle = jnp.concatenate([left_side[:, None], cells, right_side[:, None]], axis=1)
    return jnp.concatenate([upper[None], middle, lower[None]], axis=0)


def return_border(border, maps, place, link_row, turn_row):
    intra, seam_cell, edge, _, _, rim_side, rim_pos = maps
    tiles, frame_len = intra.shape
    rim_len = frame_len - 4
    side = edge.shape[0] // 4
    exact = lax.Precision.HIGHEST
    borders = lax.all_gather(border, "tile", axis=0, tiled=True)
    seam_sum = jnp.dot(
        one_hot(jnp.arange(4 * side), jnp.asarray(seam_cell.reshape(-1)), jnp.float32),
        borders,
        precision=exact,
    )
    seam_set = lax.all_gather(seam_sum, "face", axis=0, tiled=True)
    own_cells = place * rim_len + jnp.arange(rim_len)
    from_tiles = jnp.dot(
        one_hot(own_cells, jnp.asarray(intra.reshape(-1)), jnp.float32), borders, precision=exact
    )
    pick = lambda table: lax.dynamic_index_in_dim(jnp.asarray(table), place, 0, False)
    glued = seam_source(pick(rim_side), pick(rim_pos), link_row, turn_row, side)
    from_seams = jnp.dot(
        one_hot(glued, jnp.arange(seam_set.shape[0]), jnp.float32), seam_set, precision=exact
    )
    return from_tiles + from_seams


def unfold(padded, height, breadth):
    depth = padded.shape[2]
    windows = []
    for down_step in range(3):
        for side_step in range(3):
            windows.append(
                padded[down_step : down_step + height, side_step : side_step + breadth].reshape(
                    height * breadth, depth
                )
            )
    return jnp.concatenate(windows, axis=1)


def grad_one_size(frame):
    return (frame.shape[0] - 2) * (frame.shape[1] - 2) * frame.shape[2]


def gather_all(block, faces):
    local = lax.all_gather(block, "tile", axis=0, tiled=True)
    parts = [local]
    for shift in range(1, faces):
        pairs = [(i, (i + shift) % faces) for i in range(faces)]
        parts.append(lax.ppermute(local, "face", pairs))
    return jnp.concatenate(parts, axis=0)


def body(inputs, upstream, weight_in, weight_out, seam_link, seam_turn):
    cells = inputs[0, 0]
    height, breadth, width_in = cells.shape
    width_out = weight_out.shape[3]
    tiles = lax.axis_size("tile")
    place = lax.axis_index("tile")
    face_pos = lax.axis_index("face")
    link_row = lax.dynamic_index_in_dim(seam_link, face_pos, 0, False)
    turn_row = lax.dynamic_index_in_dim(seam_turn, face_pos, 0, False)
    maps = face_maps(tiles, height, breadth)
    source = halo_source(maps, place, link_row, turn_row)
    padded_tile_in = padded_tile(cells, maps, source)
    unfolded_in = unfold(padded_tile_in, height, breadth)
    pre_one = jnp.dot(
        unfolded_in, weight_in.reshape(-1, width_out), preferred_element_type=jnp.float32
    )
    act = gelu_value(pre_one).astype(jnp.bfloat16)
    padded_act = padded_tile(act.reshape(height, breadth, width_out), maps, source)
    unfolded_act = unfold(padded_act, height, breadth)
    kernel_out = weight_out.reshape(-1, width_out)
    pre_two = jnp.dot(unfolded_act, kernel_out, preferred_element_type=jnp.float32)
    grad_two = (upstream[0, 0].reshape(-1, width_out) * gelu_slope(pre_two)).astype(jnp.bfloat16)
    grad_w_out = lax.dot_general(
        unfolded_act, grad_two, (((0,), (0,)), ((), ())), preferred_element_type=jnp.float32
    )
    spread = lax.dot_general(
        grad_two, kernel_out, (((1,), (1,)), ((), ())), preferred_element_type=jnp.float32
    )
    frame = jnp.zeros((height + 2, breadth + 2, width_out), jnp.float32)
    for down_step in range(3):
        for side_step in range(3):
            offset = (down_step * 3 + side_step) * width_out
            piece = spread[:, offset : offset + width_out].reshape(height, breadth, width_out)
            frame = frame + jnp.pad(
                piece, ((down_step, 2 - down_step), (side_step, 2 - side_step), (0, 0))
            )
    def grad_hidden_of(frame):
        own_rim = return_border(border_of(frame), maps, place, link_row, turn_row)
        _, rim_back = jax.vjp(rim_of, jnp.zeros((height, breadth, width_out), jnp.float32))
        (rim_add,) = rim_back(own_rim)
        grad_act = frame[1:-1, 1:-1] + rim_add
        slope = gelu_slope(pre_one.reshape(height, breadth, width_out))
        return (grad_act * slope).astype(jnp.bfloat16)

    faces = lax.axis_size("face")
    gathered = faces * tiles * (padded_tile_in.size + grad_one_size(frame)) * 2
    if gathered <= factor_budget:
        total_out = lax.psum(grad_w_out, ("face", "tile"))

        def rest(frame):
            grad_one = grad_hidden_of(frame)
            every_pad = gather_all(padded_tile_in[None], faces)
            every_grad = gather_all(grad_one.reshape(1, -1, width_out), faces)
            every_grad = every_grad.reshape(-1, width_out)
            blocks = []
            for down_step in range(3):
                for side_step in range(3):
                    window = every_pad[:, down_step : down_step + height, side_step : side_step + breadth]
                    blocks.append(
                        lax.dot_general(
                            window.reshape(-1, width_in),
                            every_grad,
                            (((0,), (0,)), ((), ())),
                            preferred_element_type=jnp.float32,
                        )
                    )
            return grad_one, jnp.concatenate(blocks, axis=0)

        def skipped(frame):
            return (
                jnp.zeros((height, breadth, width_out), jnp.bfloat16),
                jnp.zeros((9 * width_in, width_out), jnp.float32),
            )

        grad_one, total_in = lax.cond(place < tiles, rest, skipped, frame)
    else:
        grad_one = grad_hidden_of(frame)
        grad_w_in = lax.dot_general(
            unfolded_in,
            grad_one.reshape(-1, width_out),
            (((0,), (0,)), ((), ())),
            preferred_element_type=jnp.float32,
        )
        size_in = grad_w_in.shape[0]
        total = lax.psum(jnp.concatenate([grad_w_in, grad_w_out], axis=0), ("face", "tile"))
        total_in = total[:size_in]
        total_out = total[size_in:]
    update_in, update_out = pl.pallas_call(
        scale_kernel,
        out_shape=(
            jax.ShapeDtypeStruct(total_in.shape, jnp.bfloat16),
            jax.ShapeDtypeStruct(total_out.shape, jnp.bfloat16),
        ),
    )(total_in, total_out)
    update_in = update_in.reshape(3, 3, width_in, width_out)
    update_out = update_out.reshape(3, 3, width_out, width_out)
    return (grad_one[None, None], update_in, update_out)


def solution(mesh):
    placed = (
        P("face", "tile", None, None, None),
        P("face", "tile", None, None, None),
        P(),
        P(),
        P(),
        P(),
    )
    return jax.shard_map(
        body,
        mesh=mesh,
        in_specs=placed,
        out_specs=(P("face", "tile", None, None, None), P(), P()),
        check_vma=False,
    )
```

```python
import numpy as np
import jax
import jax.numpy as jnp
from jax import lax
from jax.sharding import PartitionSpec as P
from jax.experimental import pallas as pl

root_half = 0.7071067811865476
inv_root_tau = 0.3989422804014327
epsilon = 1e-06
factor_budget = 48 * 2**20


def scale_kernel(in_ref, out_ref, update_in_ref, update_out_ref):
    grad_in = in_ref[...]
    grad_out = out_ref[...]
    squares = jnp.sum(grad_in * grad_in, axis=(0, 1), keepdims=True) + jnp.sum(
        grad_out * grad_out, axis=(0, 1), keepdims=True
    )
    factor = lax.rsqrt(squares / (grad_in.size + grad_out.size) + epsilon)
    update_in_ref[...] = (grad_in * factor).astype(update_in_ref.dtype)
    update_out_ref[...] = (grad_out * factor).astype(update_out_ref.dtype)


def gelu_value(pre):
    return pre * 0.5 * (1.0 + lax.erf(pre * root_half))


def gelu_slope(pre):
    return 0.5 * (1.0 + lax.erf(pre * root_half)) + pre * jnp.exp(-0.5 * pre * pre) * inv_root_tau


def rim_of(cells):
    return jnp.concatenate([cells[0], cells[-1], cells[:, 0], cells[:, -1]], axis=0)


def border_of(frame):
    return jnp.concatenate([frame[0], frame[-1], frame[1:-1, 0], frame[1:-1, -1]], axis=0)


def rim_index(li, lj, height, breadth):
    return np.where(
        li == 0,
        lj,
        np.where(
            li == height - 1,
            breadth + lj,
            np.where(lj == 0, 2 * breadth + li, 2 * breadth + height + li),
        ),
    )


def face_maps(tiles, height, breadth):
    across = tiles // 4
    side = across * breadth
    rim_len = 2 * (height + breadth)
    a = np.array([0] * (breadth + 2) + [height + 1] * (breadth + 2) + list(range(1, height + 1)) * 2)
    b = np.array(list(range(breadth + 2)) * 2 + [0] * height + [breadth + 1] * height)
    t = np.arange(tiles)
    i = (t // across)[:, None] * height - 1 + a[None, :]
    j = (t % across)[:, None] * breadth - 1 + b[None, :]
    out_i = (i < 0) | (i >= side)
    out_j = (j < 0) | (j >= side)
    inside = ~out_i & ~out_j
    seam = out_i ^ out_j
    ci = np.clip(i, 0, side - 1)
    cj = np.clip(j, 0, side - 1)
    owner = (ci // height) * across + cj // breadth
    intra = np.where(inside, owner * rim_len + rim_index(ci % height, cj % breadth, height, breadth), -1)
    s = np.where(i < 0, 0, np.where(i >= side, 1, np.where(j < 0, 2, 3)))
    p = np.where(out_i, cj, ci)
    seam_cell = np.where(seam, s * side + p, -1)
    pos = np.arange(side)
    ei = np.concatenate([np.zeros(side, int), np.full(side, side - 1), pos, pos])
    ej = np.concatenate([pos, pos, np.zeros(side, int), np.full(side, side - 1)])
    sides = np.repeat(np.arange(4), side)
    li = ei % height
    lj = ej % breadth
    k = np.where(sides == 0, lj, np.where(sides == 1, breadth + lj, np.where(sides == 2, 2 * breadth + li, 2 * breadth + height + li)))
    edge = ((ei // height) * across + ej // breadth) * rim_len + k
    edge_of_rim = np.full((tiles, rim_len), -1)
    edge_of_rim[edge // rim_len, edge % rim_len] = np.arange(4 * side)
    rim_side = np.where(edge_of_rim >= 0, edge_of_rim // side, -1)
    rim_pos = np.where(edge_of_rim >= 0, edge_of_rim % side, 0)
    frame_side = np.where(seam, s, -1)
    frame_pos = np.where(seam, p, 0)
    maps = (intra, seam_cell, edge, frame_side, frame_pos, rim_side, rim_pos)
    return tuple(m.astype(np.int32) for m in maps)


def one_hot(rows, cols, dtype):
    return (rows[:, None] == cols[None, :]).astype(dtype)


def seam_source(which, pos, link_row, turn_row, side):
    hit = which[:, None] == jnp.arange(4, dtype=which.dtype)[None, :]
    link = jnp.sum(jnp.where(hit, link_row[None, :], 0), axis=1)
    turn = jnp.sum(jnp.where(hit, turn_row[None, :], 0), axis=1)
    glued = link * side + jnp.where(turn == 1, side - 1 - pos, pos)
    return jnp.where(which >= 0, glued, -1)


def halo_source(maps, place, link_row, turn_row):
    intra, _, edge, frame_side, frame_pos, _, _ = maps
    tiles, frame_len = intra.shape
    rim_len = frame_len - 4
    side = edge.shape[0] // 4
    pick = lambda table: lax.dynamic_index_in_dim(jnp.asarray(table), place, 0, False)
    glued = seam_source(pick(frame_side), pick(frame_pos), link_row, turn_row, side)
    own_intra = pick(intra)
    return jnp.where(own_intra >= 0, own_intra, jnp.where(glued >= 0, tiles * rim_len + glued, -1))


def padded_tile(cells, maps, source):
    height, breadth, depth = cells.shape
    intra, seam_cell, edge = maps[:3]
    rim_len = 2 * (height + breadth)
    tiles = intra.shape[0]
    side = edge.shape[0] // 4
    rims = lax.all_gather(rim_of(cells), "tile", axis=0, tiled=True)
    edges = jnp.dot(
        one_hot(jnp.asarray(edge), jnp.arange(tiles * rim_len), cells.dtype),
        rims,
        preferred_element_type=jnp.float32,
    ).astype(cells.dtype)
    faces = lax.axis_size("face")
    parts = [edges]
    for shift in range(1, faces):
        pairs = [(i, (i + shift) % faces) for i in range(faces)]
        parts.append(lax.ppermute(edges, "face", pairs))
    pool = jnp.concatenate([rims] + parts, axis=0)
    halo = jnp.dot(
        one_hot(source, jnp.arange(pool.shape[0]), cells.dtype),
        pool,
        preferred_element_type=jnp.float32,
    ).astype(cells.dtype)
    upper = halo[: breadth + 2]
    lower = halo[breadth + 2 : 2 * breadth + 4]
    left_side = halo[2 * breadth + 4 : 2 * breadth + 4 + height]
    right_side = halo[2 * breadth + 4 + height :]
    middle = jnp.concatenate([left_side[:, None], cells, right_side[:, None]], axis=1)
    return jnp.concatenate([upper[None], middle, lower[None]], axis=0)


def return_border(border, maps, place, link_row, turn_row):
    intra, seam_cell, edge, _, _, rim_side, rim_pos = maps
    tiles, frame_len = intra.shape
    rim_len = frame_len - 4
    side = edge.shape[0] // 4
    exact = lax.Precision.HIGHEST
    borders = lax.all_gather(border, "tile", axis=0, tiled=True)
    seam_sum = jnp.dot(
        one_hot(jnp.arange(4 * side), jnp.asarray(seam_cell.reshape(-1)), jnp.float32),
        borders,
        precision=exact,
    )
    seam_set = lax.all_gather(seam_sum, "face", axis=0, tiled=True)
    own_cells = place * rim_len + jnp.arange(rim_len)
    from_tiles = jnp.dot(
        one_hot(own_cells, jnp.asarray(intra.reshape(-1)), jnp.float32), borders, precision=exact
    )
    pick = lambda table: lax.dynamic_index_in_dim(jnp.asarray(table), place, 0, False)
    glued = seam_source(pick(rim_side), pick(rim_pos), link_row, turn_row, side)
    from_seams = jnp.dot(
        one_hot(glued, jnp.arange(seam_set.shape[0]), jnp.float32), seam_set, precision=exact
    )
    return from_tiles + from_seams


def unfold(padded, height, breadth):
    depth = padded.shape[2]
    windows = []
    for down_step in range(3):
        for side_step in range(3):
            windows.append(
                padded[down_step : down_step + height, side_step : side_step + breadth].reshape(
                    height * breadth, depth
                )
            )
    return jnp.concatenate(windows, axis=1)


def grad_one_size(frame):
    return (frame.shape[0] - 2) * (frame.shape[1] - 2) * frame.shape[2]


def gather_all(block, faces):
    local = lax.all_gather(block, "tile", axis=0, tiled=True)
    parts = [local]
    for shift in range(1, faces):
        pairs = [(i, (i + shift) % faces) for i in range(faces)]
        parts.append(lax.ppermute(local, "face", pairs))
    return jnp.concatenate(parts, axis=0)


def body(inputs, upstream, weight_in, weight_out, seam_link, seam_turn):
    cells = inputs[0, 0]
    height, breadth, width_in = cells.shape
    width_out = weight_out.shape[3]
    tiles = lax.axis_size("tile")
    place = lax.axis_index("tile")
    face_pos = lax.axis_index("face")
    link_row = lax.dynamic_index_in_dim(seam_link, face_pos, 0, False)
    turn_row = lax.dynamic_index_in_dim(seam_turn, face_pos, 0, False)
    maps = face_maps(tiles, height, breadth)
    faces = lax.axis_size("face")
    offset_row = ((face_pos - link_row // 4) % faces) * 4 + link_row % 4
    source = halo_source(maps, place, offset_row, turn_row)
    padded_tile_in = padded_tile(cells, maps, source)
    unfolded_in = unfold(padded_tile_in, height, breadth)
    pre_one = jnp.dot(
        unfolded_in, weight_in.reshape(-1, width_out), preferred_element_type=jnp.float32
    )
    act = gelu_value(pre_one).astype(jnp.bfloat16)
    padded_act = padded_tile(act.reshape(height, breadth, width_out), maps, source)
    unfolded_act = unfold(padded_act, height, breadth)
    kernel_out = weight_out.reshape(-1, width_out)
    pre_two = jnp.dot(unfolded_act, kernel_out, preferred_element_type=jnp.float32)
    grad_two = (upstream[0, 0].reshape(-1, width_out) * gelu_slope(pre_two)).astype(jnp.bfloat16)
    grad_w_out = lax.dot_general(
        unfolded_act, grad_two, (((0,), (0,)), ((), ())), preferred_element_type=jnp.float32
    )
    spread = lax.dot_general(
        grad_two, kernel_out, (((1,), (1,)), ((), ())), preferred_element_type=jnp.float32
    )
    frame = jnp.zeros((height + 2, breadth + 2, width_out), jnp.float32)
    for down_step in range(3):
        for side_step in range(3):
            offset = (down_step * 3 + side_step) * width_out
            piece = spread[:, offset : offset + width_out].reshape(height, breadth, width_out)
            frame = frame + jnp.pad(
                piece, ((down_step, 2 - down_step), (side_step, 2 - side_step), (0, 0))
            )
    def grad_hidden_of(frame):
        own_rim = return_border(border_of(frame), maps, place, link_row, turn_row)
        _, rim_back = jax.vjp(rim_of, jnp.zeros((height, breadth, width_out), jnp.float32))
        (rim_add,) = rim_back(own_rim)
        grad_act = frame[1:-1, 1:-1] + rim_add
        slope = gelu_slope(pre_one.reshape(height, breadth, width_out))
        return (grad_act * slope).astype(jnp.bfloat16)

    faces = lax.axis_size("face")
    gathered = faces * tiles * (padded_tile_in.size + grad_one_size(frame)) * 2
    if gathered <= factor_budget:
        total_out = lax.psum(grad_w_out, ("face", "tile"))

        def rest(frame):
            grad_one = grad_hidden_of(frame)
            every_pad = gather_all(padded_tile_in[None], faces)
            every_grad = gather_all(grad_one.reshape(1, -1, width_out), faces)
            every_grad = every_grad.reshape(-1, width_out)
            blocks = []
            for down_step in range(3):
                for side_step in range(3):
                    window = every_pad[:, down_step : down_step + height, side_step : side_step + breadth]
                    blocks.append(
                        lax.dot_general(
                            window.reshape(-1, width_in),
                            every_grad,
                            (((0,), (0,)), ((), ())),
                            preferred_element_type=jnp.float32,
                        )
                    )
            return grad_one, jnp.concatenate(blocks, axis=0)

        def skipped(frame):
            return (
                jnp.zeros((height, breadth, width_out), jnp.bfloat16),
                jnp.zeros((9 * width_in, width_out), jnp.float32),
            )

        grad_one, total_in = lax.cond(place < tiles, rest, skipped, frame)
    else:
        grad_one = grad_hidden_of(frame)
        grad_w_in = lax.dot_general(
            unfolded_in,
            grad_one.reshape(-1, width_out),
            (((0,), (0,)), ((), ())),
            preferred_element_type=jnp.float32,
        )
        size_in = grad_w_in.shape[0]
        total = lax.psum(jnp.concatenate([grad_w_in, grad_w_out], axis=0), ("face", "tile"))
        total_in = total[:size_in]
        total_out = total[size_in:]
    update_in, update_out = pl.pallas_call(
        scale_kernel,
        out_shape=(
            jax.ShapeDtypeStruct(total_in.shape, jnp.bfloat16),
            jax.ShapeDtypeStruct(total_out.shape, jnp.bfloat16),
        ),
    )(total_in, total_out)
    update_in = update_in.reshape(3, 3, width_in, width_out)
    update_out = update_out.reshape(3, 3, width_out, width_out)
    return (grad_one[None, None], update_in, update_out)


def solution(mesh):
    placed = (
        P("face", "tile", None, None, None),
        P("face", "tile", None, None, None),
        P(),
        P(),
        P(),
        P(),
    )
    return jax.shard_map(
        body,
        mesh=mesh,
        in_specs=placed,
        out_specs=(P("face", "tile", None, None, None), P(), P()),
        check_vma=False,
    )
```
